32 devices in a mesh: row: 4 (over y, core), col: 8 (over z, x).
Axes of the slice: x: 2, y: 2, z: 4, core: 2. Of those that a mesh axis runs over, the one named last changes fastest.
Arguments:
- node_feats: bfloat16 [8192, 256], P(('row', 'col')), may hold values from -6 to 6
- weight: bfloat16 [256, 256], replicated, may hold values from -0.375 to 0.375
- cotangent: bfloat16 [8192, 256], P(('row', 'col')), may hold values from -6 to 6
- band_tiles: bfloat16 [384, 128, 128], P(('row', 'col')), may hold values from 0 to 0.049804688
- band_coords: int32 [384, 2], P(('row', 'col')), may hold values from 0 to 5, as said below
- bound_tiles: bfloat16 [1280, 128, 128], P(('row', 'col')), may hold values from 0 to 0.049804688
- bound_coords: int32 [1280, 2], P(('row', 'col')), may hold values from 0 to 7, as said below
- bound_count: int32 [32], P(('row', 'col')), may hold values from 0 to 40, as said below
- recv_lists: int32 [32, 8], P(('row', 'col')), may hold values from -1 to 1, as said below
- send_lists: int32 [32, 8], P(('row', 'col')), may hold values from -1 to 1, as said below
- reorder: int32 [32, 256], P(('row', 'col')), may hold values from 0 to 255, each once within a row
Outputs:
- node_out: bfloat16 [8192, 256], P(('row', 'col'))
- feat_grad: bfloat16 [8192, 256], P(('row', 'col'))
- weight_grad: float32 [256, 256], replicated
The draws below stay inside these ranges and needn't reach their ends.
Inputs may be any that keep to these rules, and one draw needn't show every extreme that they name: recv_lists[r * 8 + c, s] is a row block of device r * 8 + s, below 2, or -1 for none; it is -1 where s = c. In every row group one device receives a block from every other column. send_lists[r * 8 + s, c] equals recv_lists[r * 8 + c, s]. bound_count[d] is at least the number of entries of recv_lists[d] that are not -1; in every row group one device has all 40 slots live. `bound_coords`: pairs (row block below 2, owner column below 8); for k < bound_count[d] the owner column s of slot k has recv_lists[d, s] >= 0, and every such column is named by one of them; slots from bound_count[d] on are not used. `band_coords`: pairs (row block below 2, extended column block below (768) / 128); no pair twice on one device. `reorder`: each row is a permutation.
All inputs are finite; a program needn't handle non-finite values.
Results may differ from the reference program's by a relative error of at most 0.0095.
Values may be sent and summed in bfloat16 or wider, within the bound.
No kernel may reach another device: no remote copies, remote signals or barrier semaphores. Data moves between devices by JAX's collectives and lax.ppermute only.
A program may use at most 64 MiB of HBM per device.

```python
import jax
import jax.numpy as jnp
from jax import lax

F = 256
TILE = 128
RD = 256
BW = 256
KT = 40
BT = 12
NODES = 8192
N_ROW = 4
N_COL = 8
DEVICES = 32


def boundary_plan(key):
    base_key = jax.random.fold_in(key, 11)
    key_hot, key_live, key_block, key_extra = jax.random.split(base_key, 4)
    hottest = jax.random.randint(key_hot, (N_ROW,), 0, N_COL)
    chance = jax.random.randint(key_live, (N_ROW, N_COL, N_COL), 0, 20)
    dest_col = jnp.arange(N_COL, dtype=jnp.int32)[None, :, None]
    owner_col = jnp.arange(N_COL, dtype=jnp.int32)[None, None, :]
    is_hot = dest_col == hottest[:, None, None]
    is_live = ((chance < 9) | is_hot) & (dest_col != owner_col)
    blocks = jax.random.randint(key_block, (N_ROW, N_COL, N_COL), 0, RD // TILE)
    wanted = jnp.where(is_live, blocks, -1).astype(jnp.int32)
    live_total = jnp.sum(is_live.astype(jnp.int32), axis=2)
    surplus = jax.random.randint(key_extra, (N_ROW, N_COL), 0, 1 << 20) % (live_total + 1)
    hot_device = hottest[:, None] == jnp.arange(N_COL, dtype=jnp.int32)[None, :]
    tile_count = jnp.where(hot_device, KT, jnp.minimum(live_total + surplus, KT)).astype(jnp.int32)
    return (wanted, is_live, tile_count)


def draw_recv_lists(key, part):
    wanted, is_live, tile_count = boundary_plan(key)
    return wanted.reshape(N_ROW * N_COL, N_COL)


def draw_send_lists(key, part):
    wanted, is_live, tile_count = boundary_plan(key)
    return jnp.transpose(wanted, (0, 2, 1)).reshape(N_ROW * N_COL, N_COL)


def draw_bound_count(key, part):
    wanted, is_live, tile_count = boundary_plan(key)
    return tile_count.reshape(N_ROW * N_COL)


def draw_bound_coords(key, part):
    wanted, is_live, tile_count = boundary_plan(key)
    flat_live = is_live.reshape(N_ROW * N_COL, N_COL)
    live_total = jnp.sum(flat_live.astype(jnp.int32), axis=1)
    scores = (1 - flat_live.astype(jnp.int32)) * N_COL + jnp.arange(N_COL, dtype=jnp.int32)[None, :]
    ranking = jnp.argsort(scores, axis=1, stable=True).astype(jnp.int32)
    tile_index = jnp.arange(KT, dtype=jnp.int32)
    cycled = tile_index[None, :] % jnp.maximum(live_total, 1)[:, None]
    slots = jnp.take_along_axis(ranking, cycled, axis=1)
    row_blocks = jax.random.randint(jax.random.fold_in(key, 13), (N_ROW * N_COL, KT), 0, RD // TILE)
    return jnp.stack([row_blocks, slots], axis=-1).reshape(N_ROW * N_COL * KT, 2).astype(jnp.int32)


def draw_band_coords(key, part):
    col_tiles = RD // TILE + 2 * (BW // TILE)
    positions = RD // TILE * col_tiles
    device_keys = jax.random.split(jax.random.fold_in(key, 17), N_ROW * N_COL)

    def pick_positions(subkey):
        return jax.random.permutation(subkey, positions)[:BT]
    chosen = jax.vmap(pick_positions)(device_keys).astype(jnp.int32)
    return jnp.stack([chosen // col_tiles, chosen % col_tiles], axis=-1).reshape(N_ROW * N_COL * BT, 2).astype(jnp.int32)


def block_scale(stream_key, dims, cuts, low, high):
    def one(position, blocks):
        steps = jax.random.uniform(jax.random.fold_in(jax.random.fold_in(stream_key, 6), position), (blocks,), jnp.float32, low / len(cuts), high / len(cuts))
        return jnp.repeat(jnp.exp(steps), dims[position] // blocks).reshape((-1,) + (1,) * (len(dims) - position - 1))

    gain = one(*cuts[0])
    for cut in cuts[1:]:
        gain = gain * one(*cut)
    return gain


def scatter_about(key, extent, scale, reach, pieces=(), held_as=jnp.bfloat16):
    values = scale * jax.random.normal(key, extent, jnp.float32)
    if pieces:
        values = values * block_scale(key, extent, pieces, -0.22, 0.18)
    return jnp.clip(values, -reach, reach).astype(held_as)


def setup_inputs(seed: int = 0) -> dict:
    key_list = jax.random.split(jax.random.key(seed), 12)
    node_feats = scatter_about(key_list[0], (NODES, F), 1.0, 6.0, ((0, 32),))
    weight = scatter_about(key_list[1], (F, F), F ** -0.5, 0.375)
    cotangent = scatter_about(key_list[2], (NODES, F), 1.0, 6.0, ((0, 32),))
    band_tiles = jnp.clip(0.049804688 * jax.random.uniform(key_list[3], (DEVICES * BT, TILE, TILE), jnp.float32) ** block_scale(key_list[3], (DEVICES * BT, TILE, TILE), ((0, 32),), -0.2, 0.2), 0.0, 0.049804688).astype(jnp.bfloat16)
    band_coords = draw_band_coords(jax.random.fold_in(key_list[11], 71), 0)
    bound_tiles = jnp.clip(0.049804688 * jax.random.uniform(key_list[5], (DEVICES * KT, TILE, TILE), jnp.float32) ** block_scale(key_list[5], (DEVICES * KT, TILE, TILE), ((0, 32),), -0.2, 0.2), 0.0, 0.049804688).astype(jnp.bfloat16)
    bound_coords = draw_bound_coords(jax.random.fold_in(key_list[11], 71), 0)
    bound_count = draw_bound_count(jax.random.fold_in(key_list[11], 71), 0)
    recv_lists = draw_recv_lists(jax.random.fold_in(key_list[11], 71), 0)
    send_lists = draw_send_lists(jax.random.fold_in(key_list[11], 71), 0)
    reorder = jax.vmap(lambda own: jax.random.permutation(own, RD))(jax.random.split(key_list[10], DEVICES)).reshape((DEVICES, RD)).astype(jnp.int32)
    return dict(node_feats=node_feats, weight=weight, cotangent=cotangent, band_tiles=band_tiles, band_coords=band_coords, bound_tiles=bound_tiles, bound_coords=bound_coords, bound_count=bound_count, recv_lists=recv_lists, send_lists=send_lists, reorder=reorder)


def silu_slope(mixed, grad_band):
    sigma = jax.nn.sigmoid(mixed)
    return grad_band * sigma * (1.0 + mixed * (1.0 - sigma))


def scatter_rows(values, order):
    return jnp.zeros_like(values).at[order].set(values)


def reference(node_feats, weight, cotangent, band_tiles, band_coords, bound_tiles, bound_coords, bound_count, recv_lists, send_lists, reorder):
    devices_all = N_ROW * N_COL
    tile_rows = RD // TILE
    rim_tiles = BW // TILE
    col_tiles = tile_rows + 2 * rim_tiles
    x_band = jnp.take_along_axis(node_feats.reshape(devices_all, RD, F), reorder[:, :, None], axis=1)
    g_band = jnp.take_along_axis(cotangent.reshape(devices_all, RD, F), reorder[:, :, None], axis=1)
    hidden = jnp.dot(x_band.reshape(NODES, F), weight, preferred_element_type=jnp.float32).astype(jnp.bfloat16).reshape(devices_all, RD, F)
    band_stack = band_tiles.reshape(devices_all, BT, TILE, TILE)
    band_where = band_coords.reshape(devices_all, BT, 2)
    bound_stack = bound_tiles.reshape(devices_all, KT, TILE, TILE)
    bound_where = bound_coords.reshape(devices_all, KT, 2)
    device_ids = jnp.arange(devices_all, dtype=jnp.int32)
    col_range = jnp.arange(N_COL, dtype=jnp.int32)
    slot_range = jnp.arange(KT, dtype=jnp.int32)

    def neighbours(device):
        row_index = device // N_COL
        col_index = device % N_COL
        lower = ((row_index + N_ROW - 1) % N_ROW) * N_COL + col_index
        upper = ((row_index + 1) % N_ROW) * N_COL + col_index
        return row_index, col_index, lower, upper

    def forward_one(item):
        device, tiles_a, where_a, tiles_b, where_b, live_count, wanted = item
        row_index, col_index, lower, upper = neighbours(device)
        extended = jnp.concatenate([hidden[lower][RD - BW:], hidden[device], hidden[upper][:BW]], axis=0).reshape(col_tiles, TILE, F)
        terms_a = jnp.einsum("kab,kbf->kaf", tiles_a.astype(jnp.float32), extended[where_a[:, 1]].astype(jnp.float32))
        summed = jnp.zeros((tile_rows, TILE, F), jnp.float32).at[where_a[:, 0]].add(terms_a)
        group = lax.dynamic_slice_in_dim(hidden, row_index * N_COL, N_COL, 0).reshape(N_COL, tile_rows, TILE, F)
        picked = group[col_range, jnp.maximum(wanted, 0)]
        picked = jnp.where((wanted >= 0)[:, None, None], picked, jnp.zeros((), picked.dtype))
        terms_b = jnp.einsum("kab,kbf->kaf", tiles_b.astype(jnp.float32), picked[where_b[:, 1]].astype(jnp.float32))
        live_tiles = slot_range < live_count
        terms_b = jnp.where(live_tiles[:, None, None], terms_b, jnp.zeros((), terms_b.dtype))
        summed = summed.at[where_b[:, 0]].add(terms_b)
        return summed.reshape(RD, F)

    mixed = lax.map(forward_one, (device_ids, band_stack, band_where, bound_stack, bound_where, bound_count, recv_lists))
    out_band = jax.nn.silu(mixed).astype(jnp.bfloat16)
    node_out = jax.vmap(scatter_rows)(out_band, reorder)
    slope = silu_slope(mixed, g_band.astype(jnp.float32)).astype(jnp.bfloat16)

    def backward_one(carry, item):
        device, tiles_a, where_a, tiles_b, where_b, live_count = item
        row_index, col_index, lower, upper = neighbours(device)
        slope_blocks = slope[device].reshape(tile_rows, TILE, F)
        back_a = jnp.einsum("kab,kaf->kbf", tiles_a.astype(jnp.float32), slope_blocks[where_a[:, 0]].astype(jnp.float32))
        spread = jnp.zeros((col_tiles, TILE, F), jnp.float32).at[where_a[:, 1]].add(back_a)
        below = lax.optimization_barrier(spread[:rim_tiles].astype(jnp.bfloat16)).astype(jnp.float32)
        above = lax.optimization_barrier(spread[rim_tiles + tile_rows:].astype(jnp.bfloat16)).astype(jnp.float32)
        carry = carry.at[device].add(spread[rim_tiles:rim_tiles + tile_rows])
        carry = carry.at[lower, tile_rows - rim_tiles:].add(below)
        carry = carry.at[upper, :rim_tiles].add(above)
        back_b = jnp.einsum("kab,kaf->kbf", tiles_b.astype(jnp.float32), slope_blocks[where_b[:, 0]].astype(jnp.float32))
        live_tiles = slot_range < live_count
        back_b = jnp.where(live_tiles[:, None, None], back_b, jnp.zeros((), back_b.dtype))
        per_owner = jnp.zeros((N_COL, TILE, F), jnp.float32).at[where_b[:, 1]].add(back_b)
        per_owner = lax.optimization_barrier(per_owner.astype(jnp.bfloat16)).astype(jnp.float32)
        owners = row_index * N_COL + col_range
        given = send_lists[owners, col_index]
        per_owner = jnp.where((given >= 0)[:, None, None], per_owner, jnp.zeros((), per_owner.dtype))
        carry = carry.at[owners, jnp.maximum(given, 0)].add(per_owner)
        return carry, None

    start = jnp.zeros((devices_all, tile_rows, TILE, F), jnp.float32)
    grad_hidden, _ = lax.scan(backward_one, start, (device_ids, band_stack, band_where, bound_stack, bound_where, bound_count))
    grad_round = grad_hidden.reshape(NODES, F).astype(jnp.bfloat16)
    weight_grad = lax.dot_general(x_band.reshape(NODES, F), grad_round, (((0,), (0,)), ((), ())), preferred_element_type=jnp.float32) * (NODES ** -0.5)
    feat_band = lax.dot_general(grad_round, weight, (((1,), (1,)), ((), ())), preferred_element_type=jnp.float32).astype(jnp.bfloat16)
    feat_grad = jax.vmap(scatter_rows)(feat_band.reshape(devices_all, RD, F), reorder)
    return node_out.reshape(NODES, F), feat_grad.reshape(NODES, F), weight_grad
```

```python
import jax
import jax.numpy as jnp
from jax import lax
from jax.sharding import PartitionSpec as P

BW = 256


def padded_2(cells, sides, width):
    for axis, dim in sides:
        count = lax.axis_size(axis)
        head = lax.slice_in_dim(cells, 0, width, axis=dim)
        tail = lax.slice_in_dim(cells, cells.shape[dim] - width, cells.shape[dim], axis=dim)
        cells = jnp.concatenate(
            [
                lax.ppermute(tail, axis, [(i, (i + 1) % count) for i in range(count)]),
                cells,
                lax.ppermute(head, axis, [((i + 1) % count, i) for i in range(count)]),
            ],
            axis=dim,
        )
    return cells


def split_sum(selector, terms):
    high_part = terms.astype(jnp.bfloat16)
    low_part = (terms - high_part.astype(jnp.float32)).astype(jnp.bfloat16)
    pick = selector.astype(jnp.bfloat16)
    upper_sum = jnp.einsum("rk,kaf->raf", pick, high_part, preferred_element_type=jnp.float32)
    lower_sum = jnp.einsum("rk,kaf->raf", pick, low_part, preferred_element_type=jnp.float32)
    return upper_sum + lower_sum


def spread_sum(value, axes):
    count = lax.axis_size(axes)
    pieces = value.reshape(count, value.size // count)
    gathered = lax.all_to_all(pieces, axes, 0, 0, tiled=True)
    owned = jnp.sum(gathered.reshape(count, 1, value.size // count), axis=0)
    copies = jnp.broadcast_to(owned, (count, value.size // count))
    return lax.all_to_all(copies, axes, 0, 0, tiled=True).reshape(value.shape)


def on_device(
    node_feats,
    weight,
    cotangent,
    band_tiles,
    band_coords,
    bound_tiles,
    bound_coords,
    bound_count,
    recv_lists,
    send_lists,
    reorder,
):
    tile_size = band_tiles.shape[1]
    row_count = node_feats.shape[0]
    width_feat = node_feats.shape[1]
    tile_rows = row_count // tile_size
    rim_tiles = BW // tile_size
    col_tiles = tile_rows + 2 * rim_tiles
    ext_count = row_count + 2 * BW
    peers = lax.axis_size("col")
    slot_total = bound_tiles.shape[0]
    order = reorder[0]
    inverse = (
        jnp.zeros((row_count,), jnp.int32).at[order].set(jnp.arange(row_count, dtype=jnp.int32))
    )
    x_band = jnp.take(node_feats, order, axis=0)
    hidden = jnp.dot(x_band, weight, preferred_element_type=jnp.float32).astype(jnp.bfloat16)
    band_row_ids = band_coords[:, 0]
    band_col_ids = band_coords[:, 1]
    band_dense = jnp.zeros((tile_rows, tile_size, col_tiles, tile_size), jnp.bfloat16)
    band_dense = (
        band_dense.at[band_row_ids, :, band_col_ids].set(band_tiles).reshape(row_count, ext_count)
    )
    extended = padded_2(hidden, (("row", 0),), BW)
    mixed = jnp.dot(band_dense, extended, preferred_element_type=jnp.float32)
    blocks = hidden.reshape(tile_rows, tile_size, width_feat)
    giving = send_lists[0]
    outgoing = jnp.where(
        (giving >= 0)[:, None, None],
        jnp.take(blocks, jnp.maximum(giving, 0), axis=0),
        jnp.zeros((), jnp.bfloat16),
    )
    arrived = lax.all_to_all(outgoing, "col", split_axis=0, concat_axis=0, tiled=True)
    tile_range = jnp.arange(tile_rows, dtype=jnp.int32)
    live_slots = jnp.arange(slot_total, dtype=jnp.int32) < bound_count[0]
    bound_row_ids = bound_coords[:, 0]
    bound_owner = bound_coords[:, 1]
    bound_onehot = (bound_row_ids[None, :] == tile_range[:, None]) & live_slots[None, :]
    slot_rows = jnp.take(arrived, bound_owner, axis=0).reshape(slot_total * tile_size, width_feat)
    placed = jnp.einsum(
        "rk,kab->rakb",
        bound_onehot.astype(jnp.bfloat16),
        bound_tiles,
        preferred_element_type=jnp.bfloat16,
    )
    placed = placed.reshape(row_count, slot_total * tile_size)
    mixed = mixed + jnp.dot(placed, slot_rows, preferred_element_type=jnp.float32)
    out_band = jax.nn.silu(mixed).astype(jnp.bfloat16)
    node_out = jnp.take(out_band, inverse, axis=0)
    grad_band = jnp.take(cotangent, order, axis=0).astype(jnp.float32)
    sigma = jax.nn.sigmoid(mixed)
    slope = (grad_band * sigma * (1.0 + mixed * (1.0 - sigma))).astype(jnp.bfloat16)
    slope_blocks = slope.reshape(tile_rows, tile_size, width_feat)
    ext_grad = lax.dot_general(
        band_dense, slope, (((0,), (0,)), ((), ())), preferred_element_type=jnp.float32
    )
    rim_terms = jnp.concatenate([ext_grad[:BW], ext_grad[BW + row_count :]], axis=0).astype(
        jnp.bfloat16
    )
    padded = padded_2(rim_terms, (("row", 0),), BW)
    grad_hidden = ext_grad[BW : BW + row_count]
    grad_hidden = grad_hidden.at[:BW].add(padded[:BW].astype(jnp.float32))
    grad_hidden = grad_hidden.at[row_count - BW :].add(padded[3 * BW :].astype(jnp.float32))
    slot_back = jnp.einsum(
        "kab,kaf->kbf",
        bound_tiles,
        jnp.take(slope_blocks, bound_row_ids, axis=0),
        preferred_element_type=jnp.float32,
    )
    owner_range = jnp.arange(peers, dtype=jnp.int32)
    owner_onehot = (bound_owner[None, :] == owner_range[:, None]) & live_slots[None, :]
    to_owner = split_sum(owner_onehot, slot_back).astype(jnp.bfloat16)
    returned = lax.all_to_all(to_owner, "col", split_axis=0, concat_axis=0, tiled=True)
    block_onehot = (giving[None, :] == tile_range[:, None]).astype(jnp.bfloat16)
    from_peers = jnp.einsum(
        "bs,saf->baf", block_onehot, returned, preferred_element_type=jnp.float32
    )
    grad_hidden = grad_hidden + from_peers.reshape(row_count, width_feat)
    grad_round = grad_hidden.astype(jnp.bfloat16)
    partial_weight = lax.dot_general(
        x_band, grad_round, (((0,), (0,)), ((), ())), preferred_element_type=jnp.float32
    )
    nodes_all = row_count * lax.axis_size("row") * peers
    weight_grad = spread_sum(partial_weight, ("row", "col")) * nodes_all ** (-0.5)
    feat_band = lax.dot_general(
        grad_round, weight, (((1,), (1,)), ((), ())), preferred_element_type=jnp.float32
    ).astype(jnp.bfloat16)
    feat_grad = jnp.take(feat_band, inverse, axis=0)
    return (node_out, feat_grad, weight_grad)


def solution(mesh):
    in_specs = (
        P(("row", "col"), None),
        P(),
        P(("row", "col"), None),
        P(("row", "col"), None, None),
        P(("row", "col"), None),
        P(("row", "col"), None, None),
        P(("row", "col"), None),
        P(("row", "col")),
        P(("row", "col"), None),
        P(("row", "col"), None),
        P(("row", "col"), None),
    )
    out_specs = (P(("row", "col"), None), P(("row", "col"), None), P())
    return jax.shard_map(
        on_device, mesh=mesh, in_specs=in_specs, out_specs=out_specs, check_vma=False
    )
```

```python
import jax
import jax.numpy as jnp
from jax import lax
from jax.sharding import PartitionSpec as P

BW = 256


def padded_2(cells, sides, width):
    for axis, dim in sides:
        count = lax.axis_size(axis)
        head = lax.slice_in_dim(cells, 0, width, axis=dim)
        tail = lax.slice_in_dim(cells, cells.shape[dim] - width, cells.shape[dim], axis=dim)
        cells = jnp.concatenate(
            [
                lax.ppermute(tail, axis, [(i, (i + 1) % count) for i in range(count)]),
                cells,
                lax.ppermute(head, axis, [((i + 1) % count, i) for i in range(count)]),
            ],
            axis=dim,
        )
    return cells


def spread_sum(value, axes):
    count = lax.axis_size(axes)
    pieces = value.reshape(count, value.size // count)
    gathered = lax.all_to_all(pieces, axes, 0, 0, tiled=True)
    owned = jnp.sum(gathered.reshape(count, 1, value.size // count), axis=0)
    copies = jnp.broadcast_to(owned, (count, value.size // count))
    return lax.all_to_all(copies, axes, 0, 0, tiled=True).reshape(value.shape)


def on_device(
    node_feats,
    weight,
    cotangent,
    band_tiles,
    band_coords,
    bound_tiles,
    bound_coords,
    bound_count,
    recv_lists,
    send_lists,
    reorder,
):
    tile_size = band_tiles.shape[1]
    row_count = node_feats.shape[0]
    width_feat = node_feats.shape[1]
    tile_rows = row_count // tile_size
    rim_tiles = BW // tile_size
    col_tiles = tile_rows + 2 * rim_tiles
    ext_count = row_count + 2 * BW
    peers = lax.axis_size("col")
    slot_total = bound_tiles.shape[0]
    order = reorder[0]
    inverse = (
        jnp.zeros((row_count,), jnp.int32).at[order].set(jnp.arange(row_count, dtype=jnp.int32))
    )
    x_band = jnp.take(node_feats, order, axis=0)
    hidden = jnp.dot(x_band, weight, preferred_element_type=jnp.float32).astype(jnp.bfloat16)
    band_row_ids = band_coords[:, 0]
    band_col_ids = band_coords[:, 1]
    band_onehot = (
        (band_row_ids[:, None, None] == jnp.arange(tile_rows, dtype=jnp.int32)[None, :, None])
        & (band_col_ids[:, None, None] == jnp.arange(col_tiles, dtype=jnp.int32)[None, None, :])
    ).astype(jnp.bfloat16)
    band_dense = (
        jnp.einsum("krc,kab->racb", band_onehot, band_tiles, preferred_element_type=jnp.float32)
        .astype(jnp.bfloat16)
        .reshape(row_count, ext_count)
    )
    extended = padded_2(hidden, (("row", 0),), BW)
    mixed = jnp.dot(band_dense, extended, preferred_element_type=jnp.float32)
    blocks = hidden.reshape(tile_rows, tile_size, width_feat)
    giving = send_lists[0]
    outgoing = jnp.where(
        (giving >= 0)[:, None, None],
        jnp.take(blocks, jnp.maximum(giving, 0), axis=0),
        jnp.zeros((), jnp.bfloat16),
    )
    arrived = lax.all_to_all(outgoing, "col", split_axis=0, concat_axis=0, tiled=True)
    tile_range = jnp.arange(tile_rows, dtype=jnp.int32)
    owner_range = jnp.arange(peers, dtype=jnp.int32)
    live_slots = jnp.arange(slot_total, dtype=jnp.int32) < bound_count[0]
    bound_row_ids = bound_coords[:, 0]
    bound_owner = bound_coords[:, 1]
    slot_onehot = (
        (bound_row_ids[:, None, None] == tile_range[None, :, None])
        & (bound_owner[:, None, None] == owner_range[None, None, :])
        & live_slots[:, None, None]
    ).astype(jnp.bfloat16)
    bound_dense = jnp.einsum(
        "krs,kab->rasb", slot_onehot, bound_tiles, preferred_element_type=jnp.float32
    ).reshape(row_count, peers * tile_size)
    dense_high = bound_dense.astype(jnp.bfloat16)
    dense_low = (bound_dense - dense_high.astype(jnp.float32)).astype(jnp.bfloat16)
    arrived_rows = arrived.reshape(peers * tile_size, width_feat)
    mixed = mixed + jnp.dot(dense_high, arrived_rows, preferred_element_type=jnp.float32)
    mixed = mixed + jnp.dot(dense_low, arrived_rows, preferred_element_type=jnp.float32)
    out_band = jax.nn.silu(mixed).astype(jnp.bfloat16)
    node_out = jnp.take(out_band, inverse, axis=0)
    grad_band = jnp.take(cotangent, order, axis=0).astype(jnp.float32)
    sigma = jax.nn.sigmoid(mixed)
    slope = (grad_band * sigma * (1.0 + mixed * (1.0 - sigma))).astype(jnp.bfloat16)
    ext_grad = lax.dot_general(
        band_dense, slope, (((0,), (0,)), ((), ())), preferred_element_type=jnp.float32
    )
    rim_terms = jnp.concatenate([ext_grad[:BW], ext_grad[BW + row_count :]], axis=0).astype(
        jnp.bfloat16
    )
    padded = padded_2(rim_terms, (("row", 0),), BW)
    grad_hidden = ext_grad[BW : BW + row_count]
    grad_hidden = grad_hidden.at[:BW].add(padded[:BW].astype(jnp.float32))
    grad_hidden = grad_hidden.at[row_count - BW :].add(padded[3 * BW :].astype(jnp.float32))
    contract_rows = (((0,), (0,)), ((), ()))
    owner_terms = lax.dot_general(
        dense_high, slope, contract_rows, preferred_element_type=jnp.float32
    ) + lax.dot_general(dense_low, slope, contract_rows, preferred_element_type=jnp.float32)
    to_owner = owner_terms.astype(jnp.bfloat16).reshape(peers, tile_size, width_feat)
    returned = lax.all_to_all(to_owner, "col", split_axis=0, concat_axis=0, tiled=True)
    block_onehot = (giving[None, :] == tile_range[:, None]).astype(jnp.bfloat16)
    from_peers = jnp.einsum(
        "bs,saf->baf", block_onehot, returned, preferred_element_type=jnp.float32
    )
    grad_hidden = grad_hidden + from_peers.reshape(row_count, width_feat)
    grad_round = grad_hidden.astype(jnp.bfloat16)
    partial_weight = lax.dot_general(
        x_band, grad_round, (((0,), (0,)), ((), ())), preferred_element_type=jnp.float32
    )
    nodes_all = row_count * lax.axis_size("row") * peers
    weight_grad = spread_sum(partial_weight, ("row", "col")) * nodes_all ** (-0.5)
    feat_band = lax.dot_general(
        grad_round, weight, (((1,), (1,)), ((), ())), preferred_element_type=jnp.float32
    ).astype(jnp.bfloat16)
    feat_grad = jnp.take(feat_band, inverse, axis=0)
    return (node_out, feat_grad, weight_grad)


def solution(mesh):
    in_specs = (
        P(("row", "col"), None),
        P(),
        P(("row", "col"), None),
        P(("row", "col"), None, None),
        P(("row", "col"), None),
        P(("row", "col"), None, None),
        P(("row", "col"), None),
        P(("row", "col")),
        P(("row", "col"), None),
        P(("row", "col"), None),
        P(("row", "col"), None),
    )
    out_specs = (P(("row", "col"), None), P(("row", "col"), None), P())
    return jax.shard_map(
        on_device, mesh=mesh, in_specs=in_specs, out_specs=out_specs, check_vma=False
    )
```

```python
import jax
import jax.numpy as jnp
from jax import lax
from jax.sharding import PartitionSpec as P

BW = 256


def padded_2(cells, sides, width):
    for axis, dim in sides:
        count = lax.axis_size(axis)
        head = lax.slice_in_dim(cells, 0, width, axis=dim)
        tail = lax.slice_in_dim(cells, cells.shape[dim] - width, cells.shape[dim], axis=dim)
        cells = jnp.concatenate(
            [
                lax.ppermute(tail, axis, [(i, (i + 1) % count) for i in range(count)]),
                cells,
                lax.ppermute(head, axis, [((i + 1) % count, i) for i in range(count)]),
            ],
            axis=dim,
        )
    return cells


def spread_sum(value, axes):
    count = lax.axis_size(axes)
    pieces = value.reshape(count, value.size // count)
    gathered = lax.all_to_all(pieces, axes, 0, 0, tiled=True)
    owned = jnp.sum(gathered.reshape(count, 1, value.size // count), axis=0)
    copies = jnp.broadcast_to(owned, (count, value.size // count))
    return lax.all_to_all(copies, axes, 0, 0, tiled=True).reshape(value.shape)


def on_device(
    node_feats,
    weight,
    cotangent,
    band_tiles,
    band_coords,
    bound_tiles,
    bound_coords,
    bound_count,
    recv_lists,
    send_lists,
    reorder,
):
    tile_size = band_tiles.shape[1]
    row_count = node_feats.shape[0]
    width_feat = node_feats.shape[1]
    tile_rows = row_count // tile_size
    rim_tiles = BW // tile_size
    col_tiles = tile_rows + 2 * rim_tiles
    ext_count = row_count + 2 * BW
    peers = lax.axis_size("col")
    slot_total = bound_tiles.shape[0]
    order = reorder[0]
    inverse = (
        jnp.zeros((row_count,), jnp.int32).at[order].set(jnp.arange(row_count, dtype=jnp.int32))
    )
    x_band = jnp.take(node_feats, order, axis=0)
    hidden = jnp.dot(x_band, weight, preferred_element_type=jnp.float32).astype(jnp.bfloat16)
    band_row_ids = band_coords[:, 0]
    band_col_ids = band_coords[:, 1]
    band_onehot = (
        (band_row_ids[:, None, None] == jnp.arange(tile_rows, dtype=jnp.int32)[None, :, None])
        & (band_col_ids[:, None, None] == jnp.arange(col_tiles, dtype=jnp.int32)[None, None, :])
    ).astype(jnp.bfloat16)
    band_dense = (
        jnp.einsum("krc,kab->racb", band_onehot, band_tiles, preferred_element_type=jnp.float32)
        .astype(jnp.bfloat16)
        .reshape(row_count, ext_count)
    )
    extended = padded_2(hidden, (("row", 0),), BW)
    mixed = jnp.dot(band_dense, extended, preferred_element_type=jnp.float32)
    blocks = hidden.reshape(tile_rows, tile_size, width_feat)
    giving = send_lists[0]
    here = lax.axis_index("col")
    shifts = jnp.arange(1, peers, dtype=jnp.int32)
    giving_rel = jnp.take(giving, (here + shifts) % peers)
    outgoing = jnp.where(
        (giving_rel >= 0)[:, None, None],
        jnp.take(blocks, jnp.maximum(giving_rel, 0), axis=0),
        jnp.zeros((), jnp.bfloat16),
    )
    arrived = jnp.stack(
        [
            lax.ppermute(outgoing[k - 1], "col", [(i, (i + k) % peers) for i in range(peers)])
            for k in range(1, peers)
        ]
    )
    tile_range = jnp.arange(tile_rows, dtype=jnp.int32)
    live_slots = jnp.arange(slot_total, dtype=jnp.int32) < bound_count[0]
    bound_row_ids = bound_coords[:, 0]
    bound_shift = (here - bound_coords[:, 1]) % peers
    slot_onehot = (
        (bound_row_ids[:, None, None] == tile_range[None, :, None])
        & (bound_shift[:, None, None] == shifts[None, None, :])
        & live_slots[:, None, None]
    ).astype(jnp.bfloat16)
    bound_dense = jnp.einsum(
        "krs,kab->rasb", slot_onehot, bound_tiles, preferred_element_type=jnp.float32
    ).reshape(row_count, (peers - 1) * tile_size)
    dense_high = bound_dense.astype(jnp.bfloat16)
    dense_low = (bound_dense - dense_high.astype(jnp.float32)).astype(jnp.bfloat16)
    arrived_rows = arrived.reshape((peers - 1) * tile_size, width_feat)
    mixed = mixed + jnp.dot(dense_high, arrived_rows, preferred_element_type=jnp.float32)
    mixed = mixed + jnp.dot(dense_low, arrived_rows, preferred_element_type=jnp.float32)
    out_band = jax.nn.silu(mixed).astype(jnp.bfloat16)
    node_out = jnp.take(out_band, inverse, axis=0)
    grad_band = jnp.take(cotangent, order, axis=0).astype(jnp.float32)
    sigma = jax.nn.sigmoid(mixed)
    slope = (grad_band * sigma * (1.0 + mixed * (1.0 - sigma))).astype(jnp.bfloat16)
    ext_grad = lax.dot_general(
        band_dense, slope, (((0,), (0,)), ((), ())), preferred_element_type=jnp.float32
    )
    rim_terms = jnp.concatenate([ext_grad[:BW], ext_grad[BW + row_count :]], axis=0).astype(
        jnp.bfloat16
    )
    padded = padded_2(rim_terms, (("row", 0),), BW)
    grad_hidden = ext_grad[BW : BW + row_count]
    grad_hidden = grad_hidden.at[:BW].add(padded[:BW].astype(jnp.float32))
    grad_hidden = grad_hidden.at[row_count - BW :].add(padded[3 * BW :].astype(jnp.float32))
    contract_rows = (((0,), (0,)), ((), ()))
    owner_terms = lax.dot_general(
        dense_high, slope, contract_rows, preferred_element_type=jnp.float32
    ) + lax.dot_general(dense_low, slope, contract_rows, preferred_element_type=jnp.float32)
    to_owner = owner_terms.astype(jnp.bfloat16).reshape(peers - 1, tile_size, width_feat)
    returned = jnp.stack(
        [
            lax.ppermute(to_owner[k - 1], "col", [((i + k) % peers, i) for i in range(peers)])
            for k in range(1, peers)
        ]
    )
    block_onehot = (giving_rel[None, :] == tile_range[:, None]).astype(jnp.bfloat16)
    from_peers = jnp.einsum(
        "bs,saf->baf", block_onehot, returned, preferred_element_type=jnp.float32
    )
    grad_hidden = grad_hidden + from_peers.reshape(row_count, width_feat)
    grad_round = grad_hidden.astype(jnp.bfloat16)
    partial_weight = lax.dot_general(
        x_band, grad_round, (((0,), (0,)), ((), ())), preferred_element_type=jnp.float32
    )
    nodes_all = row_count * lax.axis_size("row") * peers
    weight_grad = spread_sum(partial_weight, ("row", "col")) * nodes_all ** (-0.5)
    feat_band = lax.dot_general(
        grad_round, weight, (((1,), (1,)), ((), ())), preferred_element_type=jnp.float32
    ).astype(jnp.bfloat16)
    feat_grad = jnp.take(feat_band, inverse, axis=0)
    return (node_out, feat_grad, weight_grad)


def solution(mesh):
    in_specs = (
        P(("row", "col"), None),
        P(),
        P(("row", "col"), None),
        P(("row", "col"), None, None),
        P(("row", "col"), None),
        P(("row", "col"), None, None),
        P(("row", "col"), None),
        P(("row", "col")),
        P(("row", "col"), None),
        P(("row", "col"), None),
        P(("row", "col"), None),
    )
    out_specs = (P(("row", "col"), None), P(("row", "col"), None), P())
    return jax.shard_map(
        on_device, mesh=mesh, in_specs=in_specs, out_specs=out_specs, check_vma=False
    )
```

```python
import jax
import jax.numpy as jnp
from jax import lax
from jax.sharding import PartitionSpec as P

BW = 256


def padded_2(cells, sides, width):
    for axis, dim in sides:
        count = lax.axis_size(axis)
        head = lax.slice_in_dim(cells, 0, width, axis=dim)
        tail = lax.slice_in_dim(cells, cells.shape[dim] - width, cells.shape[dim], axis=dim)
        cells = jnp.concatenate(
            [
                lax.ppermute(tail, axis, [(i, (i + 1) % count) for i in range(count)]),
                cells,
                lax.ppermute(head, axis, [((i + 1) % count, i) for i in range(count)]),
            ],
            axis=dim,
        )
    return cells


def spread_sum(value, axes):
    count = lax.axis_size(axes)
    pieces = value.reshape(count, value.size // count)
    gathered = lax.all_to_all(pieces, axes, 0, 0, tiled=True)
    owned = jnp.sum(gathered.reshape(count, 1, value.size // count), axis=0)
    copies = jnp.broadcast_to(owned, (count, value.size // count))
    return lax.all_to_all(copies, axes, 0, 0, tiled=True).reshape(value.shape)


def on_device(
    node_feats,
    weight,
    cotangent,
    band_tiles,
    band_coords,
    bound_tiles,
    bound_coords,
    bound_count,
    recv_lists,
    send_lists,
    reorder,
):
    tile_size = band_tiles.shape[1]
    row_count = node_feats.shape[0]
    width_feat = node_feats.shape[1]
    tile_rows = row_count // tile_size
    rim_tiles = BW // tile_size
    col_tiles = tile_rows + 2 * rim_tiles
    ext_count = row_count + 2 * BW
    peers = lax.axis_size("col")
    slot_total = bound_tiles.shape[0]
    order = reorder[0]
    inverse = (
        jnp.zeros((row_count,), jnp.int32).at[order].set(jnp.arange(row_count, dtype=jnp.int32))
    )
    x_band = jnp.take(node_feats, order, axis=0)
    hidden = jnp.dot(x_band, weight, preferred_element_type=jnp.float32).astype(jnp.bfloat16)
    band_row_ids = band_coords[:, 0]
    band_col_ids = band_coords[:, 1]
    band_onehot = (
        (band_row_ids[:, None, None] == jnp.arange(tile_rows, dtype=jnp.int32)[None, :, None])
        & (band_col_ids[:, None, None] == jnp.arange(col_tiles, dtype=jnp.int32)[None, None, :])
    ).astype(jnp.bfloat16)
    band_dense = (
        jnp.einsum("krc,kab->racb", band_onehot, band_tiles, preferred_element_type=jnp.float32)
        .astype(jnp.bfloat16)
        .reshape(row_count, ext_count)
    )
    paired = padded_2(jnp.concatenate([hidden, x_band], axis=1), (("row", 0),), BW)
    extended = paired[:, :width_feat]
    x_extended = paired[:, width_feat:]
    mixed = jnp.dot(band_dense, extended, preferred_element_type=jnp.float32)
    blocks = jnp.concatenate([hidden, x_band], axis=1).reshape(tile_rows, tile_size, 2 * width_feat)
    giving = send_lists[0]
    outgoing = jnp.where(
        (giving >= 0)[:, None, None],
        jnp.take(blocks, jnp.maximum(giving, 0), axis=0),
        jnp.zeros((), jnp.bfloat16),
    )
    arrived = lax.all_to_all(outgoing, "col", split_axis=0, concat_axis=0, tiled=True)
    tile_range = jnp.arange(tile_rows, dtype=jnp.int32)
    owner_range = jnp.arange(peers, dtype=jnp.int32)
    live_slots = jnp.arange(slot_total, dtype=jnp.int32) < bound_count[0]
    bound_row_ids = bound_coords[:, 0]
    bound_owner = bound_coords[:, 1]
    slot_onehot = (
        (bound_row_ids[:, None, None] == tile_range[None, :, None])
        & (bound_owner[:, None, None] == owner_range[None, None, :])
        & live_slots[:, None, None]
    ).astype(jnp.bfloat16)
    bound_dense = jnp.einsum(
        "krs,kab->rasb", slot_onehot, bound_tiles, preferred_element_type=jnp.float32
    ).reshape(row_count, peers * tile_size)
    dense_high = bound_dense.astype(jnp.bfloat16)
    dense_low = (bound_dense - dense_high.astype(jnp.float32)).astype(jnp.bfloat16)
    arrived_pairs = arrived.reshape(peers * tile_size, 2 * width_feat)
    arrived_rows = arrived_pairs[:, :width_feat]
    arrived_x = arrived_pairs[:, width_feat:]
    mixed = mixed + jnp.dot(dense_high, arrived_rows, preferred_element_type=jnp.float32)
    mixed = mixed + jnp.dot(dense_low, arrived_rows, preferred_element_type=jnp.float32)
    out_band = jax.nn.silu(mixed).astype(jnp.bfloat16)
    node_out = jnp.take(out_band, inverse, axis=0)
    grad_band = jnp.take(cotangent, order, axis=0).astype(jnp.float32)
    sigma = jax.nn.sigmoid(mixed)
    slope = (grad_band * sigma * (1.0 + mixed * (1.0 - sigma))).astype(jnp.bfloat16)
    ext_grad = lax.dot_general(
        band_dense, slope, (((0,), (0,)), ((), ())), preferred_element_type=jnp.float32
    )
    rim_terms = jnp.concatenate([ext_grad[:BW], ext_grad[BW + row_count :]], axis=0).astype(
        jnp.bfloat16
    )
    padded = padded_2(rim_terms, (("row", 0),), BW)
    own_terms = ext_grad[BW : BW + row_count]
    own_high = own_terms.astype(jnp.bfloat16)
    own_low = (own_terms - own_high.astype(jnp.float32)).astype(jnp.bfloat16)
    contract_rows = (((0,), (0,)), ((), ()))
    grad_hidden = ext_grad[BW : BW + row_count]
    grad_hidden = grad_hidden.at[:BW].add(padded[:BW].astype(jnp.float32))
    grad_hidden = grad_hidden.at[row_count - BW :].add(padded[3 * BW :].astype(jnp.float32))
    owner_terms = lax.dot_general(
        dense_high, slope, contract_rows, preferred_element_type=jnp.float32
    ) + lax.dot_general(dense_low, slope, contract_rows, preferred_element_type=jnp.float32)
    owner_round = owner_terms.astype(jnp.bfloat16)
    to_owner = owner_round.reshape(peers, tile_size, width_feat)
    x_rims = jnp.concatenate([x_extended[:BW], x_extended[BW + row_count :]], axis=0)
    x_own = x_extended[BW : BW + row_count]
    partial_weight = (
        lax.dot_general(x_own, own_high, contract_rows, preferred_element_type=jnp.float32)
        + lax.dot_general(x_own, own_low, contract_rows, preferred_element_type=jnp.float32)
        + lax.dot_general(x_rims, rim_terms, contract_rows, preferred_element_type=jnp.float32)
        + lax.dot_general(arrived_x, owner_round, contract_rows, preferred_element_type=jnp.float32)
    )
    returned = lax.all_to_all(to_owner, "col", split_axis=0, concat_axis=0, tiled=True)
    block_onehot = (giving[None, :] == tile_range[:, None]).astype(jnp.bfloat16)
    from_peers = jnp.einsum(
        "bs,saf->baf", block_onehot, returned, preferred_element_type=jnp.float32
    )
    grad_hidden = grad_hidden + from_peers.reshape(row_count, width_feat)
    grad_round = grad_hidden.astype(jnp.bfloat16)
    nodes_all = row_count * lax.axis_size("row") * peers
    weight_grad = spread_sum(partial_weight, ("row", "col")) * nodes_all ** (-0.5)
    feat_band = lax.dot_general(
        grad_round, weight, (((1,), (1,)), ((), ())), preferred_element_type=jnp.float32
    ).astype(jnp.bfloat16)
    feat_grad = jnp.take(feat_band, inverse, axis=0)
    return (node_out, feat_grad, weight_grad)


def solution(mesh):
    in_specs = (
        P(("row", "col"), None),
        P(),
        P(("row", "col"), None),
        P(("row", "col"), None, None),
        P(("row", "col"), None),
        P(("row", "col"), None, None),
        P(("row", "col"), None),
        P(("row", "col")),
        P(("row", "col"), None),
        P(("row", "col"), None),
        P(("row", "col"), None),
    )
    out_specs = (P(("row", "col"), None), P(("row", "col"), None), P())
    return jax.shard_map(
        on_device, mesh=mesh, in_specs=in_specs, out_specs=out_specs, check_vma=False
    )
```

```python
import jax
import jax.numpy as jnp
from jax import lax
from jax.sharding import PartitionSpec as P

BW = 256


def padded_2(cells, sides, width):
    for axis, dim in sides:
        count = lax.axis_size(axis)
        head = lax.slice_in_dim(cells, 0, width, axis=dim)
        tail = lax.slice_in_dim(cells, cells.shape[dim] - width, cells.shape[dim], axis=dim)
        cells = jnp.concatenate(
            [
                lax.ppermute(tail, axis, [(i, (i + 1) % count) for i in range(count)]),
                cells,
                lax.ppermute(head, axis, [((i + 1) % count, i) for i in range(count)]),
            ],
            axis=dim,
        )
    return cells


def spread_sum(value, axes):
    count = lax.axis_size(axes)
    pieces = value.reshape(count, value.size // count)
    gathered = lax.all_to_all(pieces, axes, 0, 0, tiled=True)
    owned = jnp.sum(gathered.reshape(count, 1, value.size // count), axis=0)
    copies = jnp.broadcast_to(owned, (count, value.size // count))
    return lax.all_to_all(copies, axes, 0, 0, tiled=True).reshape(value.shape)


def on_device(
    node_feats,
    weight,
    cotangent,
    band_tiles,
    band_coords,
    bound_tiles,
    bound_coords,
    bound_count,
    recv_lists,
    send_lists,
    reorder,
):
    tile_size = band_tiles.shape[1]
    row_count = node_feats.shape[0]
    width_feat = node_feats.shape[1]
    tile_rows = row_count // tile_size
    rim_tiles = BW // tile_size
    col_tiles = tile_rows + 2 * rim_tiles
    ext_count = row_count + 2 * BW
    peers = lax.axis_size("col")
    slot_total = bound_tiles.shape[0]
    order = reorder[0]
    node_range = jnp.arange(row_count, dtype=jnp.int32)
    band_perm = (order[:, None] == node_range[None, :]).astype(jnp.bfloat16)
    contract_rows = (((0,), (0,)), ((), ()))
    x_band = jnp.dot(band_perm, node_feats, preferred_element_type=jnp.float32).astype(
        jnp.bfloat16
    )
    hidden = jnp.dot(x_band, weight, preferred_element_type=jnp.float32).astype(jnp.bfloat16)
    band_row_ids = band_coords[:, 0]
    band_col_ids = band_coords[:, 1]
    band_onehot = (
        (band_row_ids[:, None, None] == jnp.arange(tile_rows, dtype=jnp.int32)[None, :, None])
        & (band_col_ids[:, None, None] == jnp.arange(col_tiles, dtype=jnp.int32)[None, None, :])
    ).astype(jnp.bfloat16)
    band_dense = (
        jnp.einsum("krc,kab->racb", band_onehot, band_tiles, preferred_element_type=jnp.float32)
        .astype(jnp.bfloat16)
        .reshape(row_count, ext_count)
    )
    extended = padded_2(hidden, (("row", 0),), BW)
    mixed = jnp.dot(band_dense, extended, preferred_element_type=jnp.float32)
    blocks = hidden.reshape(tile_rows, tile_size, width_feat)
    giving = send_lists[0]
    tile_range = jnp.arange(tile_rows, dtype=jnp.int32)
    give_onehot = (giving[:, None] == tile_range[None, :]).astype(jnp.bfloat16)
    outgoing = jnp.einsum(
        "sb,baf->saf", give_onehot, blocks, preferred_element_type=jnp.float32
    ).astype(jnp.bfloat16)
    arrived = lax.all_to_all(outgoing, "col", split_axis=0, concat_axis=0, tiled=True)
    owner_range = jnp.arange(peers, dtype=jnp.int32)
    live_slots = jnp.arange(slot_total, dtype=jnp.int32) < bound_count[0]
    bound_row_ids = bound_coords[:, 0]
    bound_owner = bound_coords[:, 1]
    slot_onehot = (
        (bound_row_ids[:, None, None] == tile_range[None, :, None])
        & (bound_owner[:, None, None] == owner_range[None, None, :])
        & live_slots[:, None, None]
    ).astype(jnp.bfloat16)
    bound_dense = jnp.einsum(
        "krs,kab->rasb", slot_onehot, bound_tiles, preferred_element_type=jnp.float32
    ).reshape(row_count, peers * tile_size)
    dense_high = bound_dense.astype(jnp.bfloat16)
    dense_low = (bound_dense - dense_high.astype(jnp.float32)).astype(jnp.bfloat16)
    arrived_rows = arrived.reshape(peers * tile_size, width_feat)
    mixed = mixed + jnp.dot(dense_high, arrived_rows, preferred_element_type=jnp.float32)
    mixed = mixed + jnp.dot(dense_low, arrived_rows, preferred_element_type=jnp.float32)
    out_band = jax.nn.silu(mixed).astype(jnp.bfloat16)
    node_out = lax.dot_general(
        band_perm, out_band, contract_rows, preferred_element_type=jnp.float32
    ).astype(jnp.bfloat16)
    grad_band = jnp.dot(band_perm, cotangent, preferred_element_type=jnp.float32)
    sigma = jax.nn.sigmoid(mixed)
    slope = (grad_band * sigma * (1.0 + mixed * (1.0 - sigma))).astype(jnp.bfloat16)
    ext_grad = lax.dot_general(
        band_dense, slope, (((0,), (0,)), ((), ())), preferred_element_type=jnp.float32
    )
    rim_terms = jnp.concatenate([ext_grad[:BW], ext_grad[BW + row_count :]], axis=0).astype(
        jnp.bfloat16
    )
    padded = padded_2(rim_terms, (("row", 0),), BW)
    grad_hidden = ext_grad[BW : BW + row_count]
    grad_hidden = grad_hidden.at[:BW].add(padded[:BW].astype(jnp.float32))
    grad_hidden = grad_hidden.at[row_count - BW :].add(padded[3 * BW :].astype(jnp.float32))
    owner_terms = lax.dot_general(
        dense_high, slope, contract_rows, preferred_element_type=jnp.float32
    ) + lax.dot_general(dense_low, slope, contract_rows, preferred_element_type=jnp.float32)
    to_owner = owner_terms.astype(jnp.bfloat16).reshape(peers, tile_size, width_feat)
    returned = lax.all_to_all(to_owner, "col", split_axis=0, concat_axis=0, tiled=True)
    block_onehot = (giving[None, :] == tile_range[:, None]).astype(jnp.bfloat16)
    from_peers = jnp.einsum(
        "bs,saf->baf", block_onehot, returned, preferred_element_type=jnp.float32
    )
    grad_hidden = grad_hidden + from_peers.reshape(row_count, width_feat)
    grad_round = grad_hidden.astype(jnp.bfloat16)
    partial_weight = lax.dot_general(
        x_band, grad_round, (((0,), (0,)), ((), ())), preferred_element_type=jnp.float32
    )
    nodes_all = row_count * lax.axis_size("row") * peers
    weight_grad = spread_sum(partial_weight, ("row", "col")) * nodes_all ** (-0.5)
    feat_band = lax.dot_general(
        grad_round, weight, (((1,), (1,)), ((), ())), preferred_element_type=jnp.float32
    ).astype(jnp.bfloat16)
    feat_grad = lax.dot_general(
        band_perm, feat_band, contract_rows, preferred_element_type=jnp.float32
    ).astype(jnp.bfloat16)
    return (node_out, feat_grad, weight_grad)


def solution(mesh):
    in_specs = (
        P(("row", "col"), None),
        P(),
        P(("row", "col"), None),
        P(("row", "col"), None, None),
        P(("row", "col"), None),
        P(("row", "col"), None, None),
        P(("row", "col"), None),
        P(("row", "col")),
        P(("row", "col"), None),
        P(("row", "col"), None),
        P(("row", "col"), None),
    )
    out_specs = (P(("row", "col"), None), P(("row", "col"), None), P())
    return jax.shard_map(
        on_device, mesh=mesh, in_specs=in_specs, out_specs=out_specs, check_vma=False
    )
```

```python
import jax
import jax.numpy as jnp
from jax import lax
from jax.sharding import PartitionSpec as P

BW = 256


def padded_2(cells, sides, width):
    for axis, dim in sides:
        count = lax.axis_size(axis)
        head = lax.slice_in_dim(cells, 0, width, axis=dim)
        tail = lax.slice_in_dim(cells, cells.shape[dim] - width, cells.shape[dim], axis=dim)
        cells = jnp.concatenate(
            [
                lax.ppermute(tail, axis, [(i, (i + 1) % count) for i in range(count)]),
                cells,
                lax.ppermute(head, axis, [((i + 1) % count, i) for i in range(count)]),
            ],
            axis=dim,
        )
    return cells


def spread_sum(value, axes, scale):
    count = lax.axis_size(axes)
    if value.shape[0] % count == 0:
        piece = (count, value.shape[0] // count, value.shape[1])
    else:
        piece = (count, value.size // count // 128, 128)
    gathered = lax.all_to_all(value.reshape(piece), axes, 0, 0, tiled=True)
    owned = jnp.sum(gathered, axis=0, keepdims=True) * scale
    copies = jnp.broadcast_to(owned, piece)
    return lax.all_to_all(copies, axes, 0, 0, tiled=True).reshape(value.shape)


def on_device(
    node_feats,
    weight,
    cotangent,
    band_tiles,
    band_coords,
    bound_tiles,
    bound_coords,
    bound_count,
    recv_lists,
    send_lists,
    reorder,
):
    tile_size = band_tiles.shape[1]
    row_count = node_feats.shape[0]
    width_feat = node_feats.shape[1]
    tile_rows = row_count // tile_size
    rim_tiles = BW // tile_size
    col_tiles = tile_rows + 2 * rim_tiles
    ext_count = row_count + 2 * BW
    peers = lax.axis_size("col")
    slot_total = bound_tiles.shape[0]
    order = reorder[0]
    node_range = jnp.arange(row_count, dtype=jnp.int32)
    band_perm = (order[:, None] == node_range[None, :]).astype(jnp.bfloat16)
    contract_rows = (((0,), (0,)), ((), ()))
    x_band = jnp.dot(band_perm, node_feats, preferred_element_type=jnp.float32).astype(
        jnp.bfloat16
    )
    hidden = jnp.dot(x_band, weight, preferred_element_type=jnp.float32).astype(jnp.bfloat16)
    band_row_ids = band_coords[:, 0]
    band_col_ids = band_coords[:, 1]
    band_onehot = (
        (band_row_ids[:, None, None] == jnp.arange(tile_rows, dtype=jnp.int32)[None, :, None])
        & (band_col_ids[:, None, None] == jnp.arange(col_tiles, dtype=jnp.int32)[None, None, :])
    ).astype(jnp.bfloat16)
    band_dense = (
        jnp.einsum("krc,kab->racb", band_onehot, band_tiles, preferred_element_type=jnp.float32)
        .astype(jnp.bfloat16)
        .reshape(row_count, ext_count)
    )
    extended = padded_2(hidden, (("row", 0),), BW)
    mixed = jnp.dot(band_dense, extended, preferred_element_type=jnp.float32)
    blocks = hidden.reshape(tile_rows, tile_size, width_feat)
    giving = send_lists[0]
    tile_range = jnp.arange(tile_rows, dtype=jnp.int32)
    give_onehot = (giving[:, None] == tile_range[None, :]).astype(jnp.bfloat16)
    outgoing = jnp.einsum(
        "sb,baf->saf", give_onehot, blocks, preferred_element_type=jnp.float32
    ).astype(jnp.bfloat16)
    arrived = lax.all_to_all(outgoing, "col", split_axis=0, concat_axis=0, tiled=True)
    owner_range = jnp.arange(peers, dtype=jnp.int32)
    live_slots = jnp.arange(slot_total, dtype=jnp.int32) < bound_count[0]
    bound_row_ids = bound_coords[:, 0]
    bound_owner = bound_coords[:, 1]
    slot_onehot = (
        (bound_row_ids[:, None, None] == tile_range[None, :, None])
        & (bound_owner[:, None, None] == owner_range[None, None, :])
        & live_slots[:, None, None]
    ).astype(jnp.bfloat16)
    bound_dense = jnp.einsum(
        "krs,kab->rasb", slot_onehot, bound_tiles, preferred_element_type=jnp.float32
    ).reshape(row_count, peers * tile_size)
    dense_high = bound_dense.astype(jnp.bfloat16)
    dense_low = (bound_dense - dense_high.astype(jnp.float32)).astype(jnp.bfloat16)
    arrived_rows = arrived.reshape(peers * tile_size, width_feat)
    mixed = mixed + jnp.dot(dense_high, arrived_rows, preferred_element_type=jnp.float32)
    mixed = mixed + jnp.dot(dense_low, arrived_rows, preferred_element_type=jnp.float32)
    out_band = jax.nn.silu(mixed).astype(jnp.bfloat16)
    node_out = lax.dot_general(
        band_perm, out_band, contract_rows, preferred_element_type=jnp.float32
    ).astype(jnp.bfloat16)
    grad_band = jnp.dot(band_perm, cotangent, preferred_element_type=jnp.float32)
    sigma = jax.nn.sigmoid(mixed)
    slope = (grad_band * sigma * (1.0 + mixed * (1.0 - sigma))).astype(jnp.bfloat16)
    ext_grad = lax.dot_general(
        band_dense, slope, (((0,), (0,)), ((), ())), preferred_element_type=jnp.float32
    )
    rim_terms = jnp.concatenate([ext_grad[:BW], ext_grad[BW + row_count :]], axis=0).astype(
        jnp.bfloat16
    )
    padded = padded_2(rim_terms, (("row", 0),), BW)
    grad_hidden = ext_grad[BW : BW + row_count]
    grad_hidden = grad_hidden.at[:BW].add(padded[:BW].astype(jnp.float32))
    grad_hidden = grad_hidden.at[row_count - BW :].add(padded[3 * BW :].astype(jnp.float32))
    owner_terms = lax.dot_general(
        dense_high, slope, contract_rows, preferred_element_type=jnp.float32
    ) + lax.dot_general(dense_low, slope, contract_rows, preferred_element_type=jnp.float32)
    to_owner = owner_terms.astype(jnp.bfloat16).reshape(peers, tile_size, width_feat)
    returned = lax.all_to_all(to_owner, "col", split_axis=0, concat_axis=0, tiled=True)
    block_onehot = (giving[None, :] == tile_range[:, None]).astype(jnp.bfloat16)
    from_peers = jnp.einsum(
        "bs,saf->baf", block_onehot, returned, preferred_element_type=jnp.float32
    )
    grad_hidden = grad_hidden + from_peers.reshape(row_count, width_feat)
    grad_round = grad_hidden.astype(jnp.bfloat16)
    partial_weight = lax.dot_general(
        x_band, grad_round, (((0,), (0,)), ((), ())), preferred_element_type=jnp.float32
    )
    nodes_all = row_count * lax.axis_size("row") * peers
    weight_grad = spread_sum(partial_weight, ("row", "col"), nodes_all ** (-0.5))
    feat_band = lax.dot_general(
        grad_round, weight, (((1,), (1,)), ((), ())), preferred_element_type=jnp.float32
    ).astype(jnp.bfloat16)
    feat_grad = lax.dot_general(
        band_perm, feat_band, contract_rows, preferred_element_type=jnp.float32
    ).astype(jnp.bfloat16)
    return (node_out, feat_grad, weight_grad)


def solution(mesh):
    in_specs = (
        P(("row", "col"), None),
        P(),
        P(("row", "col"), None),
        P(("row", "col"), None, None),
        P(("row", "col"), None),
        P(("row", "col"), None, None),
        P(("row", "col"), None),
        P(("row", "col")),
        P(("row", "col"), None),
        P(("row", "col"), None),
        P(("row", "col"), None),
    )
    out_specs = (P(("row", "col"), None), P(("row", "col"), None), P())
    return jax.shard_map(
        on_device, mesh=mesh, in_specs=in_specs, out_specs=out_specs, check_vma=False
    )
```

```python
import jax
import jax.numpy as jnp
from jax import lax
from jax.sharding import PartitionSpec as P

BW = 256


def padded_2(cells, sides, width):
    for axis, dim in sides:
        count = lax.axis_size(axis)
        head = lax.slice_in_dim(cells, 0, width, axis=dim)
        tail = lax.slice_in_dim(cells, cells.shape[dim] - width, cells.shape[dim], axis=dim)
        cells = jnp.concatenate(
            [
                lax.ppermute(tail, axis, [(i, (i + 1) % count) for i in range(count)]),
                cells,
                lax.ppermute(head, axis, [((i + 1) % count, i) for i in range(count)]),
            ],
            axis=dim,
        )
    return cells


def spread_sum(value, axes, scale):
    count = lax.axis_size(axes)
    if value.shape[0] % count == 0:
        piece = (count, value.shape[0] // count, value.shape[1])
    else:
        piece = (count, value.size // count // 128, 128)
    gathered = lax.all_to_all(value.reshape(piece), axes, 0, 0, tiled=True)
    owned = jnp.sum(gathered, axis=0, keepdims=True) * scale
    copies = jnp.broadcast_to(owned, piece)
    return lax.all_to_all(copies, axes, 0, 0, tiled=True).reshape(value.shape)


def on_device(
    node_feats,
    weight,
    cotangent,
    band_tiles,
    band_coords,
    bound_tiles,
    bound_coords,
    bound_count,
    recv_lists,
    send_lists,
    reorder,
):
    tile_size = band_tiles.shape[1]
    row_count = node_feats.shape[0]
    width_feat = node_feats.shape[1]
    tile_rows = row_count // tile_size
    rim_tiles = BW // tile_size
    col_tiles = tile_rows + 2 * rim_tiles
    ext_count = row_count + 2 * BW
    peers = lax.axis_size("col")
    slot_total = bound_tiles.shape[0]
    order = reorder[0]
    node_range = jnp.arange(row_count, dtype=jnp.int32)
    band_perm = (order[:, None] == node_range[None, :]).astype(jnp.bfloat16)
    contract_rows = (((0,), (0,)), ((), ()))
    x_band = jnp.dot(band_perm, node_feats, preferred_element_type=jnp.float32).astype(
        jnp.bfloat16
    )
    giving = send_lists[0]
    tile_range = jnp.arange(tile_rows, dtype=jnp.int32)
    give_onehot = (giving[:, None] == tile_range[None, :]).astype(jnp.bfloat16)
    send_pick = jnp.einsum(
        "sb,bai->sai",
        give_onehot,
        band_perm.reshape(tile_rows, tile_size, row_count),
        preferred_element_type=jnp.float32,
    ).astype(jnp.bfloat16)
    outgoing = jnp.dot(
        send_pick.reshape(peers * tile_size, row_count),
        node_feats,
        preferred_element_type=jnp.float32,
    ).astype(jnp.bfloat16)
    arrived = lax.all_to_all(
        outgoing.reshape(peers, tile_size, width_feat), "col", split_axis=0, concat_axis=0, tiled=True
    )
    band_row_ids = band_coords[:, 0]
    band_col_ids = band_coords[:, 1]
    band_onehot = (
        (band_row_ids[:, None, None] == jnp.arange(tile_rows, dtype=jnp.int32)[None, :, None])
        & (band_col_ids[:, None, None] == jnp.arange(col_tiles, dtype=jnp.int32)[None, None, :])
    ).astype(jnp.bfloat16)
    band_dense = (
        jnp.einsum("krc,kab->racb", band_onehot, band_tiles, preferred_element_type=jnp.float32)
        .astype(jnp.bfloat16)
        .reshape(row_count, ext_count)
    )
    x_extended = padded_2(x_band, (("row", 0),), BW)
    extended = jnp.dot(x_extended, weight, preferred_element_type=jnp.float32).astype(jnp.bfloat16)
    mixed = jnp.dot(band_dense, extended, preferred_element_type=jnp.float32)
    owner_range = jnp.arange(peers, dtype=jnp.int32)
    live_slots = jnp.arange(slot_total, dtype=jnp.int32) < bound_count[0]
    bound_row_ids = bound_coords[:, 0]
    bound_owner = bound_coords[:, 1]
    slot_onehot = (
        (bound_row_ids[:, None, None] == tile_range[None, :, None])
        & (bound_owner[:, None, None] == owner_range[None, None, :])
        & live_slots[:, None, None]
    ).astype(jnp.bfloat16)
    bound_dense = jnp.einsum(
        "krs,kab->rasb", slot_onehot, bound_tiles, preferred_element_type=jnp.float32
    ).reshape(row_count, peers * tile_size)
    dense_high = bound_dense.astype(jnp.bfloat16)
    dense_low = (bound_dense - dense_high.astype(jnp.float32)).astype(jnp.bfloat16)
    arrived_rows = jnp.dot(
        arrived.reshape(peers * tile_size, width_feat), weight, preferred_element_type=jnp.float32
    ).astype(jnp.bfloat16)
    mixed = mixed + jnp.dot(dense_high, arrived_rows, preferred_element_type=jnp.float32)
    mixed = mixed + jnp.dot(dense_low, arrived_rows, preferred_element_type=jnp.float32)
    out_band = jax.nn.silu(mixed).astype(jnp.bfloat16)
    node_out = lax.dot_general(
        band_perm, out_band, contract_rows, preferred_element_type=jnp.float32
    ).astype(jnp.bfloat16)
    grad_band = jnp.dot(band_perm, cotangent, preferred_element_type=jnp.float32)
    sigma = jax.nn.sigmoid(mixed)
    slope = (grad_band * sigma * (1.0 + mixed * (1.0 - sigma))).astype(jnp.bfloat16)
    ext_grad = lax.dot_general(
        band_dense, slope, (((0,), (0,)), ((), ())), preferred_element_type=jnp.float32
    )
    rim_terms = jnp.concatenate([ext_grad[:BW], ext_grad[BW + row_count :]], axis=0).astype(
        jnp.bfloat16
    )
    padded = padded_2(rim_terms, (("row", 0),), BW)
    grad_hidden = ext_grad[BW : BW + row_count]
    grad_hidden = grad_hidden.at[:BW].add(padded[:BW].astype(jnp.float32))
    grad_hidden = grad_hidden.at[row_count - BW :].add(padded[3 * BW :].astype(jnp.float32))
    owner_terms = lax.dot_general(
        dense_high, slope, contract_rows, preferred_element_type=jnp.float32
    ) + lax.dot_general(dense_low, slope, contract_rows, preferred_element_type=jnp.float32)
    to_owner = owner_terms.astype(jnp.bfloat16).reshape(peers, tile_size, width_feat)
    returned = lax.all_to_all(to_owner, "col", split_axis=0, concat_axis=0, tiled=True)
    block_onehot = (giving[None, :] == tile_range[:, None]).astype(jnp.bfloat16)
    from_peers = jnp.einsum(
        "bs,saf->baf", block_onehot, returned, preferred_element_type=jnp.float32
    )
    grad_hidden = grad_hidden + from_peers.reshape(row_count, width_feat)
    grad_round = grad_hidden.astype(jnp.bfloat16)
    partial_weight = lax.dot_general(
        x_band, grad_round, (((0,), (0,)), ((), ())), preferred_element_type=jnp.float32
    )
    nodes_all = row_count * lax.axis_size("row") * peers
    weight_grad = spread_sum(partial_weight, ("row", "col"), nodes_all ** (-0.5))
    feat_band = lax.dot_general(
        grad_round, weight, (((1,), (1,)), ((), ())), preferred_element_type=jnp.float32
    ).astype(jnp.bfloat16)
    feat_grad = lax.dot_general(
        band_perm, feat_band, contract_rows, preferred_element_type=jnp.float32
    ).astype(jnp.bfloat16)
    return (node_out, feat_grad, weight_grad)


def solution(mesh):
    in_specs = (
        P(("row", "col"), None),
        P(),
        P(("row", "col"), None),
        P(("row", "col"), None, None),
        P(("row", "col"), None),
        P(("row", "col"), None, None),
        P(("row", "col"), None),
        P(("row", "col")),
        P(("row", "col"), None),
        P(("row", "col"), None),
        P(("row", "col"), None),
    )
    out_specs = (P(("row", "col"), None), P(("row", "col"), None), P())
    return jax.shard_map(
        on_device, mesh=mesh, in_specs=in_specs, out_specs=out_specs, check_vma=False
    )
```

```python
import jax
import jax.numpy as jnp
from jax import lax
from jax.sharding import PartitionSpec as P

BW = 256


def padded_2(cells, sides, width):
    for axis, dim in sides:
        count = lax.axis_size(axis)
        head = lax.slice_in_dim(cells, 0, width, axis=dim)
        tail = lax.slice_in_dim(cells, cells.shape[dim] - width, cells.shape[dim], axis=dim)
        cells = jnp.concatenate(
            [
                lax.ppermute(tail, axis, [(i, (i + 1) % count) for i in range(count)]),
                cells,
                lax.ppermute(head, axis, [((i + 1) % count, i) for i in range(count)]),
            ],
            axis=dim,
        )
    return cells


def spread_sum(value, axes, scale):
    count = lax.axis_size(axes)
    if value.shape[0] % count == 0:
        piece = (count, value.shape[0] // count, value.shape[1])
    else:
        piece = (count, value.size // count // 128, 128)
    gathered = lax.all_to_all(value.reshape(piece), axes, 0, 0, tiled=True)
    owned = jnp.sum(gathered, axis=0, keepdims=True) * scale
    copies = jnp.broadcast_to(owned, piece)
    return lax.all_to_all(copies, axes, 0, 0, tiled=True).reshape(value.shape)


def on_device(
    node_feats,
    weight,
    cotangent,
    band_tiles,
    band_coords,
    bound_tiles,
    bound_coords,
    bound_count,
    recv_lists,
    send_lists,
    reorder,
):
    tile_size = band_tiles.shape[1]
    row_count = node_feats.shape[0]
    width_feat = node_feats.shape[1]
    tile_rows = row_count // tile_size
    rim_tiles = BW // tile_size
    col_tiles = tile_rows + 2 * rim_tiles
    ext_count = row_count + 2 * BW
    peers = lax.axis_size("col")
    slot_total = bound_tiles.shape[0]
    order = reorder[0]
    node_range = jnp.arange(row_count, dtype=jnp.int32)
    band_perm = (order[:, None] == node_range[None, :]).astype(jnp.bfloat16)
    contract_rows = (((0,), (0,)), ((), ()))
    x_band = jnp.dot(band_perm, node_feats, preferred_element_type=jnp.float32).astype(
        jnp.bfloat16
    )
    hidden = jnp.dot(x_band, weight, preferred_element_type=jnp.float32).astype(jnp.bfloat16)
    band_row_ids = band_coords[:, 0]
    band_col_ids = band_coords[:, 1]
    band_onehot = (
        (band_row_ids[:, None, None] == jnp.arange(tile_rows, dtype=jnp.int32)[None, :, None])
        & (band_col_ids[:, None, None] == jnp.arange(col_tiles, dtype=jnp.int32)[None, None, :])
    ).astype(jnp.bfloat16)
    band_dense = (
        jnp.einsum("krc,kab->racb", band_onehot, band_tiles, preferred_element_type=jnp.float32)
        .astype(jnp.bfloat16)
        .reshape(row_count, ext_count)
    )
    extended = padded_2(hidden, (("row", 0),), BW)
    mixed = jnp.dot(band_dense, extended, preferred_element_type=jnp.float32)
    giving = send_lists[0]
    tile_range = jnp.arange(tile_rows, dtype=jnp.int32)
    send_rows = jnp.where(
        giving[:, None] >= 0,
        giving[:, None] * tile_size + jnp.arange(tile_size, dtype=jnp.int32)[None, :],
        -1,
    ).reshape(peers * tile_size)
    send_pick = (send_rows[:, None] == node_range[None, :]).astype(jnp.bfloat16)
    outgoing = (
        jnp.dot(send_pick, hidden, preferred_element_type=jnp.float32)
        .astype(jnp.bfloat16)
        .reshape(peers, tile_size, width_feat)
    )
    arrived = lax.all_to_all(outgoing, "col", split_axis=0, concat_axis=0, tiled=True)
    owner_range = jnp.arange(peers, dtype=jnp.int32)
    live_slots = jnp.arange(slot_total, dtype=jnp.int32) < bound_count[0]
    bound_row_ids = bound_coords[:, 0]
    bound_owner = bound_coords[:, 1]
    slot_onehot = (
        (bound_row_ids[:, None, None] == tile_range[None, :, None])
        & (bound_owner[:, None, None] == owner_range[None, None, :])
        & live_slots[:, None, None]
    ).astype(jnp.bfloat16)
    bound_dense = jnp.einsum(
        "krs,kab->rasb", slot_onehot, bound_tiles, preferred_element_type=jnp.float32
    ).reshape(row_count, peers * tile_size)
    dense_high = bound_dense.astype(jnp.bfloat16)
    dense_low = (bound_dense - dense_high.astype(jnp.float32)).astype(jnp.bfloat16)
    arrived_rows = arrived.reshape(peers * tile_size, width_feat)
    mixed = mixed + jnp.dot(dense_high, arrived_rows, preferred_element_type=jnp.float32)
    mixed = mixed + jnp.dot(dense_low, arrived_rows, preferred_element_type=jnp.float32)
    out_band = jax.nn.silu(mixed).astype(jnp.bfloat16)
    node_out = lax.dot_general(
        band_perm, out_band, contract_rows, preferred_element_type=jnp.float32
    ).astype(jnp.bfloat16)
    grad_band = jnp.dot(band_perm, cotangent, preferred_element_type=jnp.float32)
    sigma = jax.nn.sigmoid(mixed)
    slope = (grad_band * sigma * (1.0 + mixed * (1.0 - sigma))).astype(jnp.bfloat16)
    ext_grad = lax.dot_general(
        band_dense, slope, (((0,), (0,)), ((), ())), preferred_element_type=jnp.float32
    )
    rim_terms = jnp.concatenate([ext_grad[:BW], ext_grad[BW + row_count :]], axis=0).astype(
        jnp.bfloat16
    )
    padded = padded_2(rim_terms, (("row", 0),), BW)
    grad_hidden = ext_grad[BW : BW + row_count]
    grad_hidden = grad_hidden.at[:BW].add(padded[:BW].astype(jnp.float32))
    grad_hidden = grad_hidden.at[row_count - BW :].add(padded[3 * BW :].astype(jnp.float32))
    owner_terms = lax.dot_general(
        dense_high, slope, contract_rows, preferred_element_type=jnp.float32
    ) + lax.dot_general(dense_low, slope, contract_rows, preferred_element_type=jnp.float32)
    to_owner = owner_terms.astype(jnp.bfloat16).reshape(peers, tile_size, width_feat)
    returned = lax.all_to_all(to_owner, "col", split_axis=0, concat_axis=0, tiled=True)
    block_onehot = (giving[None, :] == tile_range[:, None]).astype(jnp.bfloat16)
    from_peers = jnp.einsum(
        "bs,saf->baf", block_onehot, returned, preferred_element_type=jnp.float32
    )
    grad_hidden = grad_hidden + from_peers.reshape(row_count, width_feat)
    grad_round = grad_hidden.astype(jnp.bfloat16)
    partial_weight = lax.dot_general(
        x_band, grad_round, (((0,), (0,)), ((), ())), preferred_element_type=jnp.float32
    )
    nodes_all = row_count * lax.axis_size("row") * peers
    weight_grad = spread_sum(partial_weight, ("row", "col"), nodes_all ** (-0.5))
    feat_band = lax.dot_general(
        grad_round, weight, (((1,), (1,)), ((), ())), preferred_element_type=jnp.float32
    ).astype(jnp.bfloat16)
    feat_grad = lax.dot_general(
        band_perm, feat_band, contract_rows, preferred_element_type=jnp.float32
    ).astype(jnp.bfloat16)
    return (node_out, feat_grad, weight_grad)


def solution(mesh):
    in_specs = (
        P(("row", "col"), None),
        P(),
        P(("row", "col"), None),
        P(("row", "col"), None, None),
        P(("row", "col"), None),
        P(("row", "col"), None, None),
        P(("row", "col"), None),
        P(("row", "col")),
        P(("row", "col"), None),
        P(("row", "col"), None),
        P(("row", "col"), None),
    )
    out_specs = (P(("row", "col"), None), P(("row", "col"), None), P())
    return jax.shard_map(
        on_device, mesh=mesh, in_specs=in_specs, out_specs=out_specs, check_vma=False
    )
```

```python
import jax
import jax.numpy as jnp
from jax import lax
from jax.sharding import PartitionSpec as P

BW = 256


def padded_2(cells, sides, width):
    for axis, dim in sides:
        count = lax.axis_size(axis)
        head = lax.slice_in_dim(cells, 0, width, axis=dim)
        tail = lax.slice_in_dim(cells, cells.shape[dim] - width, cells.shape[dim], axis=dim)
        cells = jnp.concatenate(
            [
                lax.ppermute(tail, axis, [(i, (i + 1) % count) for i in range(count)]),
                cells,
                lax.ppermute(head, axis, [((i + 1) % count, i) for i in range(count)]),
            ],
            axis=dim,
        )
    return cells


def spread_sum(value, axes, scale):
    count = lax.axis_size(axes)
    if value.shape[0] % count == 0:
        piece = (count, value.shape[0] // count, value.shape[1])
    else:
        piece = (count, value.size // count // 128, 128)
    gathered = lax.all_to_all(value.reshape(piece), axes, 0, 0, tiled=True)
    owned = jnp.sum(gathered, axis=0, keepdims=True) * scale
    copies = jnp.broadcast_to(owned, piece)
    return lax.all_to_all(copies, axes, 0, 0, tiled=True).reshape(value.shape)


def on_device(
    node_feats,
    weight,
    cotangent,
    band_tiles,
    band_coords,
    bound_tiles,
    bound_coords,
    bound_count,
    recv_lists,
    send_lists,
    reorder,
):
    tile_size = band_tiles.shape[1]
    row_count = node_feats.shape[0]
    width_feat = node_feats.shape[1]
    tile_rows = row_count // tile_size
    rim_tiles = BW // tile_size
    col_tiles = tile_rows + 2 * rim_tiles
    ext_count = row_count + 2 * BW
    peers = lax.axis_size("col")
    slot_total = bound_tiles.shape[0]
    order = reorder[0]
    node_range = jnp.arange(row_count, dtype=jnp.int32)
    band_perm = (order[:, None] == node_range[None, :]).astype(jnp.bfloat16)
    contract_rows = (((0,), (0,)), ((), ()))
    x_band = jnp.dot(band_perm, node_feats, preferred_element_type=jnp.float32).astype(
        jnp.bfloat16
    )
    band_row_ids = band_coords[:, 0]
    band_col_ids = band_coords[:, 1]
    band_onehot = (
        (band_row_ids[:, None, None] == jnp.arange(tile_rows, dtype=jnp.int32)[None, :, None])
        & (band_col_ids[:, None, None] == jnp.arange(col_tiles, dtype=jnp.int32)[None, None, :])
    ).astype(jnp.bfloat16)
    band_dense = (
        jnp.einsum("krc,kab->racb", band_onehot, band_tiles, preferred_element_type=jnp.float32)
        .astype(jnp.bfloat16)
        .reshape(row_count, ext_count)
    )
    x_extended = padded_2(x_band, (("row", 0),), BW)
    extended = jnp.dot(x_extended, weight, preferred_element_type=jnp.float32).astype(jnp.bfloat16)
    mixed = jnp.dot(band_dense, extended, preferred_element_type=jnp.float32)
    giving = send_lists[0]
    tile_range = jnp.arange(tile_rows, dtype=jnp.int32)
    send_rows = jnp.where(
        giving[:, None] >= 0,
        giving[:, None] * tile_size + jnp.arange(tile_size, dtype=jnp.int32)[None, :],
        -1,
    ).reshape(peers * tile_size)
    send_nodes = jnp.take(order, jnp.maximum(send_rows, 0))
    send_pick = ((send_nodes[:, None] == node_range[None, :]) & (send_rows[:, None] >= 0)).astype(
        jnp.bfloat16
    )
    outgoing = (
        jnp.dot(send_pick, node_feats, preferred_element_type=jnp.float32)
        .astype(jnp.bfloat16)
        .reshape(peers, tile_size, width_feat)
    )
    arrived = lax.all_to_all(outgoing, "col", split_axis=0, concat_axis=0, tiled=True)
    owner_range = jnp.arange(peers, dtype=jnp.int32)
    live_slots = jnp.arange(slot_total, dtype=jnp.int32) < bound_count[0]
    bound_row_ids = bound_coords[:, 0]
    bound_owner = bound_coords[:, 1]
    slot_onehot = (
        (bound_row_ids[:, None, None] == tile_range[None, :, None])
        & (bound_owner[:, None, None] == owner_range[None, None, :])
        & live_slots[:, None, None]
    ).astype(jnp.bfloat16)
    bound_dense = jnp.einsum(
        "krs,kab->rasb", slot_onehot, bound_tiles, preferred_element_type=jnp.float32
    ).reshape(row_count, peers * tile_size)
    dense_high = bound_dense.astype(jnp.bfloat16)
    dense_low = (bound_dense - dense_high.astype(jnp.float32)).astype(jnp.bfloat16)
    arrived_x = arrived.reshape(peers * tile_size, width_feat)
    arrived_rows = jnp.dot(arrived_x, weight, preferred_element_type=jnp.float32).astype(
        jnp.bfloat16
    )
    mixed = mixed + jnp.dot(dense_high, arrived_rows, preferred_element_type=jnp.float32)
    mixed = mixed + jnp.dot(dense_low, arrived_rows, preferred_element_type=jnp.float32)
    out_band = jax.nn.silu(mixed).astype(jnp.bfloat16)
    node_out = lax.dot_general(
        band_perm, out_band, contract_rows, preferred_element_type=jnp.float32
    ).astype(jnp.bfloat16)
    grad_band = jnp.dot(band_perm, cotangent, preferred_element_type=jnp.float32)
    sigma = jax.nn.sigmoid(mixed)
    slope = (grad_band * sigma * (1.0 + mixed * (1.0 - sigma))).astype(jnp.bfloat16)
    ext_grad = lax.dot_general(
        band_dense, slope, (((0,), (0,)), ((), ())), preferred_element_type=jnp.float32
    )
    rim_terms = jnp.concatenate([ext_grad[:BW], ext_grad[BW + row_count :]], axis=0).astype(
        jnp.bfloat16
    )
    padded = padded_2(rim_terms, (("row", 0),), BW)
    grad_hidden = ext_grad[BW : BW + row_count]
    grad_hidden = grad_hidden.at[:BW].add(padded[:BW].astype(jnp.float32))
    grad_hidden = grad_hidden.at[row_count - BW :].add(padded[3 * BW :].astype(jnp.float32))
    owner_terms = lax.dot_general(
        dense_high, slope, contract_rows, preferred_element_type=jnp.float32
    ) + lax.dot_general(dense_low, slope, contract_rows, preferred_element_type=jnp.float32)
    owner_round = owner_terms.astype(jnp.bfloat16)
    to_owner = owner_round.reshape(peers, tile_size, width_feat)
    own_terms = ext_grad[BW : BW + row_count]
    local_high = own_terms.astype(jnp.bfloat16)
    local_low = (own_terms - local_high.astype(jnp.float32)).astype(jnp.bfloat16)
    x_rims = jnp.concatenate([x_extended[:BW], x_extended[BW + row_count :]], axis=0)
    partial_weight = (
        lax.dot_general(x_band, local_high, contract_rows, preferred_element_type=jnp.float32)
        + lax.dot_general(x_band, local_low, contract_rows, preferred_element_type=jnp.float32)
        + lax.dot_general(x_rims, rim_terms, contract_rows, preferred_element_type=jnp.float32)
        + lax.dot_general(arrived_x, owner_round, contract_rows, preferred_element_type=jnp.float32)
    )
    here = lax.axis_index("col")
    returned = jnp.stack(
        [
            lax.ppermute(
                jnp.take(to_owner, (here + k) % peers, axis=0),
                "col",
                [(i, (i + k) % peers) for i in range(peers)],
            )
            for k in range(1, peers)
        ]
    )
    source_cols = (here - jnp.arange(1, peers, dtype=jnp.int32)) % peers
    back_blocks = jnp.take(giving, source_cols)
    block_onehot = (back_blocks[None, :] == tile_range[:, None]).astype(jnp.bfloat16)
    from_peers = jnp.einsum(
        "bs,saf->baf", block_onehot, returned, preferred_element_type=jnp.float32
    )
    grad_hidden = grad_hidden + from_peers.reshape(row_count, width_feat)
    grad_round = grad_hidden.astype(jnp.bfloat16)
    nodes_all = row_count * lax.axis_size("row") * peers
    weight_grad = spread_sum(partial_weight, ("row", "col"), nodes_all ** (-0.5))
    feat_band = lax.dot_general(
        grad_round, weight, (((1,), (1,)), ((), ())), preferred_element_type=jnp.float32
    ).astype(jnp.bfloat16)
    feat_grad = lax.dot_general(
        band_perm, feat_band, contract_rows, preferred_element_type=jnp.float32
    ).astype(jnp.bfloat16)
    return (node_out, feat_grad, weight_grad)


def solution(mesh):
    in_specs = (
        P(("row", "col"), None),
        P(),
        P(("row", "col"), None),
        P(("row", "col"), None, None),
        P(("row", "col"), None),
        P(("row", "col"), None, None),
        P(("row", "col"), None),
        P(("row", "col")),
        P(("row", "col"), None),
        P(("row", "col"), None),
        P(("row", "col"), None),
    )
    out_specs = (P(("row", "col"), None), P(("row", "col"), None), P())
    return jax.shard_map(
        on_device, mesh=mesh, in_specs=in_specs, out_specs=out_specs, check_vma=False
    )
```

```python
import jax
import jax.numpy as jnp
from jax import lax
from jax.sharding import PartitionSpec as P

BW = 256


def padded_2(cells, sides, width):
    for axis, dim in sides:
        count = lax.axis_size(axis)
        head = lax.slice_in_dim(cells, 0, width, axis=dim)
        tail = lax.slice_in_dim(cells, cells.shape[dim] - width, cells.shape[dim], axis=dim)
        cells = jnp.concatenate(
            [
                lax.ppermute(tail, axis, [(i, (i + 1) % count) for i in range(count)]),
                cells,
                lax.ppermute(head, axis, [((i + 1) % count, i) for i in range(count)]),
            ],
            axis=dim,
        )
    return cells


def spread_sum(value, axes, scale):
    count = lax.axis_size(axes)
    if value.shape[0] % count == 0:
        piece = (count, value.shape[0] // count, value.shape[1])
    else:
        piece = (count, value.size // count // 128, 128)
    gathered = lax.all_to_all(value.reshape(piece), axes, 0, 0, tiled=True)
    owned = jnp.sum(gathered, axis=0, keepdims=True) * scale
    copies = jnp.broadcast_to(owned, piece)
    return lax.all_to_all(copies, axes, 0, 0, tiled=True).reshape(value.shape)


def on_device(
    node_feats,
    weight,
    cotangent,
    band_tiles,
    band_coords,
    bound_tiles,
    bound_coords,
    bound_count,
    recv_lists,
    send_lists,
    reorder,
):
    tile_size = band_tiles.shape[1]
    row_count = node_feats.shape[0]
    width_feat = node_feats.shape[1]
    tile_rows = row_count // tile_size
    rim_tiles = BW // tile_size
    col_tiles = tile_rows + 2 * rim_tiles
    ext_count = row_count + 2 * BW
    peers = lax.axis_size("col")
    slot_total = bound_tiles.shape[0]
    order = reorder[0]
    node_range = jnp.arange(row_count, dtype=jnp.int32)
    band_perm = (order[:, None] == node_range[None, :]).astype(jnp.bfloat16)
    contract_rows = (((0,), (0,)), ((), ()))
    x_band = jnp.dot(band_perm, node_feats, preferred_element_type=jnp.float32).astype(
        jnp.bfloat16
    )
    hidden = jnp.dot(x_band, weight, preferred_element_type=jnp.float32).astype(jnp.bfloat16)
    band_row_ids = band_coords[:, 0]
    band_col_ids = band_coords[:, 1]
    band_onehot = (
        (band_row_ids[:, None, None] == jnp.arange(tile_rows, dtype=jnp.int32)[None, :, None])
        & (band_col_ids[:, None, None] == jnp.arange(col_tiles, dtype=jnp.int32)[None, None, :])
    ).astype(jnp.bfloat16)
    band_dense = (
        jnp.einsum("krc,kab->racb", band_onehot, band_tiles, preferred_element_type=jnp.float32)
        .astype(jnp.bfloat16)
        .reshape(row_count, ext_count)
    )
    extended = padded_2(hidden, (("row", 0),), BW)
    band_mixed = jnp.dot(band_dense, extended, preferred_element_type=jnp.float32)
    giving = send_lists[0]
    tile_range = jnp.arange(tile_rows, dtype=jnp.int32)
    send_rows = jnp.where(
        giving[:, None] >= 0,
        giving[:, None] * tile_size + jnp.arange(tile_size, dtype=jnp.int32)[None, :],
        -1,
    ).reshape(peers * tile_size)
    send_pick = (send_rows[:, None] == node_range[None, :]).astype(jnp.bfloat16)
    outgoing = (
        jnp.dot(send_pick, hidden, preferred_element_type=jnp.float32)
        .astype(jnp.bfloat16)
        .reshape(peers, tile_size, width_feat)
    )
    arrived = lax.all_to_all(outgoing, "col", split_axis=0, concat_axis=0, tiled=True)
    owner_range = jnp.arange(peers, dtype=jnp.int32)
    live_slots = jnp.arange(slot_total, dtype=jnp.int32) < bound_count[0]
    bound_row_ids = bound_coords[:, 0]
    bound_owner = bound_coords[:, 1]
    slot_onehot = (
        (bound_row_ids[:, None, None] == tile_range[None, :, None])
        & (bound_owner[:, None, None] == owner_range[None, None, :])
        & live_slots[:, None, None]
    ).astype(jnp.bfloat16)
    bound_dense = jnp.einsum(
        "krs,kab->rasb", slot_onehot, bound_tiles, preferred_element_type=jnp.float32
    ).reshape(row_count, peers * tile_size)
    dense_high = bound_dense.astype(jnp.bfloat16)
    dense_low = (bound_dense - dense_high.astype(jnp.float32)).astype(jnp.bfloat16)
    band_mixed, arrived = lax.optimization_barrier((band_mixed, arrived))
    arrived_rows = arrived.reshape(peers * tile_size, width_feat)
    mixed = band_mixed + jnp.dot(dense_high, arrived_rows, preferred_element_type=jnp.float32)
    mixed = mixed + jnp.dot(dense_low, arrived_rows, preferred_element_type=jnp.float32)
    out_band = jax.nn.silu(mixed).astype(jnp.bfloat16)
    node_out = lax.dot_general(
        band_perm, out_band, contract_rows, preferred_element_type=jnp.float32
    ).astype(jnp.bfloat16)
    grad_band = jnp.dot(band_perm, cotangent, preferred_element_type=jnp.float32)
    sigma = jax.nn.sigmoid(mixed)
    slope = (grad_band * sigma * (1.0 + mixed * (1.0 - sigma))).astype(jnp.bfloat16)
    ext_grad = lax.dot_general(
        band_dense, slope, (((0,), (0,)), ((), ())), preferred_element_type=jnp.float32
    )
    rim_terms = jnp.concatenate([ext_grad[:BW], ext_grad[BW + row_count :]], axis=0).astype(
        jnp.bfloat16
    )
    padded = padded_2(rim_terms, (("row", 0),), BW)
    grad_hidden = ext_grad[BW : BW + row_count]
    grad_hidden = grad_hidden.at[:BW].add(padded[:BW].astype(jnp.float32))
    grad_hidden = grad_hidden.at[row_count - BW :].add(padded[3 * BW :].astype(jnp.float32))
    owner_terms = lax.dot_general(
        dense_high, slope, contract_rows, preferred_element_type=jnp.float32
    ) + lax.dot_general(dense_low, slope, contract_rows, preferred_element_type=jnp.float32)
    to_owner = owner_terms.astype(jnp.bfloat16).reshape(peers, tile_size, width_feat)
    returned = lax.all_to_all(to_owner, "col", split_axis=0, concat_axis=0, tiled=True)
    block_onehot = (giving[None, :] == tile_range[:, None]).astype(jnp.bfloat16)
    from_peers = jnp.einsum(
        "bs,saf->baf", block_onehot, returned, preferred_element_type=jnp.float32
    )
    grad_hidden = grad_hidden + from_peers.reshape(row_count, width_feat)
    grad_round = grad_hidden.astype(jnp.bfloat16)
    partial_weight = lax.dot_general(
        x_band, grad_round, (((0,), (0,)), ((), ())), preferred_element_type=jnp.float32
    )
    nodes_all = row_count * lax.axis_size("row") * peers
    weight_grad = spread_sum(partial_weight, ("row", "col"), nodes_all ** (-0.5))
    feat_band = lax.dot_general(
        grad_round, weight, (((1,), (1,)), ((), ())), preferred_element_type=jnp.float32
    ).astype(jnp.bfloat16)
    feat_grad = lax.dot_general(
        band_perm, feat_band, contract_rows, preferred_element_type=jnp.float32
    ).astype(jnp.bfloat16)
    return (node_out, feat_grad, weight_grad)


def solution(mesh):
    in_specs = (
        P(("row", "col"), None),
        P(),
        P(("row", "col"), None),
        P(("row", "col"), None, None),
        P(("row", "col"), None),
        P(("row", "col"), None, None),
        P(("row", "col"), None),
        P(("row", "col")),
        P(("row", "col"), None),
        P(("row", "col"), None),
        P(("row", "col"), None),
    )
    out_specs = (P(("row", "col"), None), P(("row", "col"), None), P())
    return jax.shard_map(
        on_device, mesh=mesh, in_specs=in_specs, out_specs=out_specs, check_vma=False
    )
```

```python
import jax
import jax.numpy as jnp
from jax import lax
from jax.sharding import PartitionSpec as P

BW = 256


def padded_2(cells, sides, width):
    for axis, dim in sides:
        count = lax.axis_size(axis)
        head = lax.slice_in_dim(cells, 0, width, axis=dim)
        tail = lax.slice_in_dim(cells, cells.shape[dim] - width, cells.shape[dim], axis=dim)
        cells = jnp.concatenate(
            [
                lax.ppermute(tail, axis, [(i, (i + 1) % count) for i in range(count)]),
                cells,
                lax.ppermute(head, axis, [((i + 1) % count, i) for i in range(count)]),
            ],
            axis=dim,
        )
    return cells


def spread_sum(value, axes, scale):
    count = lax.axis_size(axes)
    if value.shape[0] % count == 0:
        piece = (count, value.shape[0] // count, value.shape[1])
    else:
        piece = (count, value.size // count // 128, 128)
    gathered = lax.all_to_all(value.reshape(piece), axes, 0, 0, tiled=True)
    owned = (jnp.sum(gathered, axis=0, keepdims=True) * scale).astype(jnp.bfloat16)
    copies = jnp.broadcast_to(owned, piece)
    spread = lax.all_to_all(copies, axes, 0, 0, tiled=True)
    return spread.astype(jnp.float32).reshape(value.shape)


def on_device(
    node_feats,
    weight,
    cotangent,
    band_tiles,
    band_coords,
    bound_tiles,
    bound_coords,
    bound_count,
    recv_lists,
    send_lists,
    reorder,
):
    tile_size = band_tiles.shape[1]
    row_count = node_feats.shape[0]
    width_feat = node_feats.shape[1]
    tile_rows = row_count // tile_size
    rim_tiles = BW // tile_size
    col_tiles = tile_rows + 2 * rim_tiles
    ext_count = row_count + 2 * BW
    peers = lax.axis_size("col")
    slot_total = bound_tiles.shape[0]
    order = reorder[0]
    node_range = jnp.arange(row_count, dtype=jnp.int32)
    band_perm = (order[:, None] == node_range[None, :]).astype(jnp.bfloat16)
    contract_rows = (((0,), (0,)), ((), ()))
    x_band = jnp.dot(band_perm, node_feats, preferred_element_type=jnp.float32).astype(
        jnp.bfloat16
    )
    hidden = jnp.dot(x_band, weight, preferred_element_type=jnp.float32).astype(jnp.bfloat16)
    band_row_ids = band_coords[:, 0]
    band_col_ids = band_coords[:, 1]
    band_onehot = (
        (band_row_ids[:, None, None] == jnp.arange(tile_rows, dtype=jnp.int32)[None, :, None])
        & (band_col_ids[:, None, None] == jnp.arange(col_tiles, dtype=jnp.int32)[None, None, :])
    ).astype(jnp.bfloat16)
    band_dense = (
        jnp.einsum("krc,kab->racb", band_onehot, band_tiles, preferred_element_type=jnp.float32)
        .astype(jnp.bfloat16)
        .reshape(row_count, ext_count)
    )
    extended = padded_2(hidden, (("row", 0),), BW)
    mixed = jnp.dot(band_dense, extended, preferred_element_type=jnp.float32)
    blocks = hidden.reshape(tile_rows, tile_size, width_feat)
    giving = send_lists[0]
    tile_range = jnp.arange(tile_rows, dtype=jnp.int32)
    give_onehot = (giving[:, None] == tile_range[None, :]).astype(jnp.bfloat16)
    outgoing = jnp.einsum(
        "sb,baf->saf", give_onehot, blocks, preferred_element_type=jnp.float32
    ).astype(jnp.bfloat16)
    arrived = lax.all_to_all(outgoing, "col", split_axis=0, concat_axis=0, tiled=True)
    owner_range = jnp.arange(peers, dtype=jnp.int32)
    live_slots = jnp.arange(slot_total, dtype=jnp.int32) < bound_count[0]
    bound_row_ids = bound_coords[:, 0]
    bound_owner = bound_coords[:, 1]
    slot_onehot = (
        (bound_row_ids[:, None, None] == tile_range[None, :, None])
        & (bound_owner[:, None, None] == owner_range[None, None, :])
        & live_slots[:, None, None]
    ).astype(jnp.bfloat16)
    bound_dense = jnp.einsum(
        "krs,kab->rasb", slot_onehot, bound_tiles, preferred_element_type=jnp.float32
    ).reshape(row_count, peers * tile_size)
    dense_high = bound_dense.astype(jnp.bfloat16)
    dense_low = (bound_dense - dense_high.astype(jnp.float32)).astype(jnp.bfloat16)
    arrived_rows = arrived.reshape(peers * tile_size, width_feat)
    mixed = mixed + jnp.dot(dense_high, arrived_rows, preferred_element_type=jnp.float32)
    mixed = mixed + jnp.dot(dense_low, arrived_rows, preferred_element_type=jnp.float32)
    out_band = jax.nn.silu(mixed).astype(jnp.bfloat16)
    node_out = lax.dot_general(
        band_perm, out_band, contract_rows, preferred_element_type=jnp.float32
    ).astype(jnp.bfloat16)
    grad_band = jnp.dot(band_perm, cotangent, preferred_element_type=jnp.float32)
    sigma = jax.nn.sigmoid(mixed)
    slope = (grad_band * sigma * (1.0 + mixed * (1.0 - sigma))).astype(jnp.bfloat16)
    ext_grad = lax.dot_general(
        band_dense, slope, (((0,), (0,)), ((), ())), preferred_element_type=jnp.float32
    )
    rim_terms = jnp.concatenate([ext_grad[:BW], ext_grad[BW + row_count :]], axis=0).astype(
        jnp.bfloat16
    )
    padded = padded_2(rim_terms, (("row", 0),), BW)
    grad_hidden = ext_grad[BW : BW + row_count]
    grad_hidden = grad_hidden.at[:BW].add(padded[:BW].astype(jnp.float32))
    grad_hidden = grad_hidden.at[row_count - BW :].add(padded[3 * BW :].astype(jnp.float32))
    owner_terms = lax.dot_general(
        dense_high, slope, contract_rows, preferred_element_type=jnp.float32
    ) + lax.dot_general(dense_low, slope, contract_rows, preferred_element_type=jnp.float32)
    to_owner = owner_terms.astype(jnp.bfloat16).reshape(peers, tile_size, width_feat)
    returned = lax.all_to_all(to_owner, "col", split_axis=0, concat_axis=0, tiled=True)
    block_onehot = (giving[None, :] == tile_range[:, None]).astype(jnp.bfloat16)
    from_peers = jnp.einsum(
        "bs,saf->baf", block_onehot, returned, preferred_element_type=jnp.float32
    )
    grad_hidden = grad_hidden + from_peers.reshape(row_count, width_feat)
    grad_round = grad_hidden.astype(jnp.bfloat16)
    partial_weight = lax.dot_general(
        x_band, grad_round, (((0,), (0,)), ((), ())), preferred_element_type=jnp.float32
    )
    nodes_all = row_count * lax.axis_size("row") * peers
    weight_grad = spread_sum(partial_weight, ("row", "col"), nodes_all ** (-0.5))
    feat_band = lax.dot_general(
        grad_round, weight, (((1,), (1,)), ((), ())), preferred_element_type=jnp.float32
    ).astype(jnp.bfloat16)
    feat_grad = lax.dot_general(
        band_perm, feat_band, contract_rows, preferred_element_type=jnp.float32
    ).astype(jnp.bfloat16)
    return (node_out, feat_grad, weight_grad)


def solution(mesh):
    in_specs = (
        P(("row", "col"), None),
        P(),
        P(("row", "col"), None),
        P(("row", "col"), None, None),
        P(("row", "col"), None),
        P(("row", "col"), None, None),
        P(("row", "col"), None),
        P(("row", "col")),
        P(("row", "col"), None),
        P(("row", "col"), None),
        P(("row", "col"), None),
    )
    out_specs = (P(("row", "col"), None), P(("row", "col"), None), P())
    return jax.shard_map(
        on_device, mesh=mesh, in_specs=in_specs, out_specs=out_specs, check_vma=False
    )
```

```python
import jax
import jax.numpy as jnp
from jax import lax
from jax.sharding import PartitionSpec as P

BW = 256


def padded_2(cells, sides, width):
    for axis, dim in sides:
        count = lax.axis_size(axis)
        head = lax.slice_in_dim(cells, 0, width, axis=dim)
        tail = lax.slice_in_dim(cells, cells.shape[dim] - width, cells.shape[dim], axis=dim)
        cells = jnp.concatenate(
            [
                lax.ppermute(tail, axis, [(i, (i + 1) % count) for i in range(count)]),
                cells,
                lax.ppermute(head, axis, [((i + 1) % count, i) for i in range(count)]),
            ],
            axis=dim,
        )
    return cells


def spread_sum(value, axes, scale):
    count = lax.axis_size(axes)
    if value.shape[0] % count == 0:
        piece = (count, value.shape[0] // count, value.shape[1])
    else:
        piece = (count, value.size // count // 128, 128)
    gathered = lax.all_to_all(value.reshape(piece), axes, 0, 0, tiled=True)
    owned = (jnp.sum(gathered, axis=0, keepdims=True) * scale).astype(jnp.bfloat16)
    narrow = (count, value.size // count // 128, 128)
    copies = jnp.broadcast_to(owned.reshape((1,) + narrow[1:]), narrow)
    spread = lax.all_to_all(copies, axes, 0, 0, tiled=True)
    return spread.astype(jnp.float32).reshape(value.shape)


def on_device(
    node_feats,
    weight,
    cotangent,
    band_tiles,
    band_coords,
    bound_tiles,
    bound_coords,
    bound_count,
    recv_lists,
    send_lists,
    reorder,
):
    tile_size = band_tiles.shape[1]
    row_count = node_feats.shape[0]
    width_feat = node_feats.shape[1]
    tile_rows = row_count // tile_size
    rim_tiles = BW // tile_size
    col_tiles = tile_rows + 2 * rim_tiles
    ext_count = row_count + 2 * BW
    peers = lax.axis_size("col")
    slot_total = bound_tiles.shape[0]
    order = reorder[0]
    node_range = jnp.arange(row_count, dtype=jnp.int32)
    band_perm = (order[:, None] == node_range[None, :]).astype(jnp.bfloat16)
    contract_rows = (((0,), (0,)), ((), ()))
    x_band = jnp.dot(band_perm, node_feats, preferred_element_type=jnp.float32).astype(
        jnp.bfloat16
    )
    hidden = jnp.dot(x_band, weight, preferred_element_type=jnp.float32).astype(jnp.bfloat16)
    band_row_ids = band_coords[:, 0]
    band_col_ids = band_coords[:, 1]
    band_onehot = (
        (band_row_ids[:, None, None] == jnp.arange(tile_rows, dtype=jnp.int32)[None, :, None])
        & (band_col_ids[:, None, None] == jnp.arange(col_tiles, dtype=jnp.int32)[None, None, :])
    ).astype(jnp.bfloat16)
    band_dense = (
        jnp.einsum("krc,kab->racb", band_onehot, band_tiles, preferred_element_type=jnp.float32)
        .astype(jnp.bfloat16)
        .reshape(row_count, ext_count)
    )
    extended = padded_2(hidden, (("row", 0),), BW)
    mixed = jnp.dot(band_dense, extended, preferred_element_type=jnp.float32)
    blocks = hidden.reshape(tile_rows, tile_size, width_feat)
    giving = send_lists[0]
    tile_range = jnp.arange(tile_rows, dtype=jnp.int32)
    give_onehot = (giving[:, None] == tile_range[None, :]).astype(jnp.bfloat16)
    outgoing = jnp.einsum(
        "sb,baf->saf", give_onehot, blocks, preferred_element_type=jnp.float32
    ).astype(jnp.bfloat16)
    arrived = lax.all_to_all(outgoing, "col", split_axis=0, concat_axis=0, tiled=True)
    owner_range = jnp.arange(peers, dtype=jnp.int32)
    live_slots = jnp.arange(slot_total, dtype=jnp.int32) < bound_count[0]
    bound_row_ids = bound_coords[:, 0]
    bound_owner = bound_coords[:, 1]
    slot_onehot = (
        (bound_row_ids[:, None, None] == tile_range[None, :, None])
        & (bound_owner[:, None, None] == owner_range[None, None, :])
        & live_slots[:, None, None]
    ).astype(jnp.bfloat16)
    bound_dense = jnp.einsum(
        "krs,kab->rasb", slot_onehot, bound_tiles, preferred_element_type=jnp.float32
    ).reshape(row_count, peers * tile_size)
    dense_high = bound_dense.astype(jnp.bfloat16)
    dense_low = (bound_dense - dense_high.astype(jnp.float32)).astype(jnp.bfloat16)
    arrived_rows = arrived.reshape(peers * tile_size, width_feat)
    mixed = mixed + jnp.dot(dense_high, arrived_rows, preferred_element_type=jnp.float32)
    mixed = mixed + jnp.dot(dense_low, arrived_rows, preferred_element_type=jnp.float32)
    out_band = jax.nn.silu(mixed).astype(jnp.bfloat16)
    node_out = lax.dot_general(
        band_perm, out_band, contract_rows, preferred_element_type=jnp.float32
    ).astype(jnp.bfloat16)
    grad_band = jnp.dot(band_perm, cotangent, preferred_element_type=jnp.float32)
    sigma = jax.nn.sigmoid(mixed)
    slope = (grad_band * sigma * (1.0 + mixed * (1.0 - sigma))).astype(jnp.bfloat16)
    ext_grad = lax.dot_general(
        band_dense, slope, (((0,), (0,)), ((), ())), preferred_element_type=jnp.float32
    )
    rim_terms = jnp.concatenate([ext_grad[:BW], ext_grad[BW + row_count :]], axis=0).astype(
        jnp.bfloat16
    )
    padded = padded_2(rim_terms, (("row", 0),), BW)
    grad_hidden = ext_grad[BW : BW + row_count]
    grad_hidden = grad_hidden.at[:BW].add(padded[:BW].astype(jnp.float32))
    grad_hidden = grad_hidden.at[row_count - BW :].add(padded[3 * BW :].astype(jnp.float32))
    owner_terms = lax.dot_general(
        dense_high, slope, contract_rows, preferred_element_type=jnp.float32
    ) + lax.dot_general(dense_low, slope, contract_rows, preferred_element_type=jnp.float32)
    to_owner = owner_terms.astype(jnp.bfloat16).reshape(peers, tile_size, width_feat)
    returned = lax.all_to_all(to_owner, "col", split_axis=0, concat_axis=0, tiled=True)
    block_onehot = (giving[None, :] == tile_range[:, None]).astype(jnp.bfloat16)
    from_peers = jnp.einsum(
        "bs,saf->baf", block_onehot, returned, preferred_element_type=jnp.float32
    )
    grad_hidden = grad_hidden + from_peers.reshape(row_count, width_feat)
    grad_round = grad_hidden.astype(jnp.bfloat16)
    partial_weight = lax.dot_general(
        x_band, grad_round, (((0,), (0,)), ((), ())), preferred_element_type=jnp.float32
    )
    nodes_all = row_count * lax.axis_size("row") * peers
    weight_grad = spread_sum(partial_weight, ("row", "col"), nodes_all ** (-0.5))
    feat_band = lax.dot_general(
        grad_round, weight, (((1,), (1,)), ((), ())), preferred_element_type=jnp.float32
    ).astype(jnp.bfloat16)
    feat_grad = lax.dot_general(
        band_perm, feat_band, contract_rows, preferred_element_type=jnp.float32
    ).astype(jnp.bfloat16)
    return (node_out, feat_grad, weight_grad)


def solution(mesh):
    in_specs = (
        P(("row", "col"), None),
        P(),
        P(("row", "col"), None),
        P(("row", "col"), None, None),
        P(("row", "col"), None),
        P(("row", "col"), None, None),
        P(("row", "col"), None),
        P(("row", "col")),
        P(("row", "col"), None),
        P(("row", "col"), None),
        P(("row", "col"), None),
    )
    out_specs = (P(("row", "col"), None), P(("row", "col"), None), P())
    return jax.shard_map(
        on_device, mesh=mesh, in_specs=in_specs, out_specs=out_specs, check_vma=False
    )
```

```python
import jax
import jax.numpy as jnp
from jax import lax
from jax.sharding import PartitionSpec as P

BW = 256


def padded_2(cells, sides, width):
    for axis, dim in sides:
        count = lax.axis_size(axis)
        head = lax.slice_in_dim(cells, 0, width, axis=dim)
        tail = lax.slice_in_dim(cells, cells.shape[dim] - width, cells.shape[dim], axis=dim)
        cells = jnp.concatenate(
            [
                lax.ppermute(tail, axis, [(i, (i + 1) % count) for i in range(count)]),
                cells,
                lax.ppermute(head, axis, [((i + 1) % count, i) for i in range(count)]),
            ],
            axis=dim,
        )
    return cells


def spread_sum(value, axes, scale):
    count = lax.axis_size(axes)
    if value.shape[0] % count == 0:
        piece = (count, value.shape[0] // count, value.shape[1])
    else:
        piece = (count, value.size // count // 128, 128)
    gathered = lax.all_to_all(value.reshape(piece), axes, 0, 0, tiled=True)
    owned = (jnp.sum(gathered, axis=0, keepdims=True) * scale).astype(jnp.bfloat16)
    copies = jnp.broadcast_to(owned, piece)
    spread = lax.all_to_all(copies, axes, 0, 0, tiled=True)
    return spread.astype(jnp.float32).reshape(value.shape)


def on_device(
    node_feats,
    weight,
    cotangent,
    band_tiles,
    band_coords,
    bound_tiles,
    bound_coords,
    bound_count,
    recv_lists,
    send_lists,
    reorder,
):
    tile_size = band_tiles.shape[1]
    row_count = node_feats.shape[0]
    width_feat = node_feats.shape[1]
    tile_rows = row_count // tile_size
    rim_tiles = BW // tile_size
    col_tiles = tile_rows + 2 * rim_tiles
    ext_count = row_count + 2 * BW
    peers = lax.axis_size("col")
    slot_total = bound_tiles.shape[0]
    order = reorder[0]
    node_range = jnp.arange(row_count, dtype=jnp.int32)
    band_perm = (order[:, None] == node_range[None, :]).astype(jnp.bfloat16)
    contract_rows = (((0,), (0,)), ((), ()))
    x_band = jnp.dot(band_perm, node_feats, preferred_element_type=jnp.float32).astype(
        jnp.bfloat16
    )
    hidden = jnp.dot(x_band, weight, preferred_element_type=jnp.float32).astype(jnp.bfloat16)
    band_row_ids = band_coords[:, 0]
    band_col_ids = band_coords[:, 1]
    band_onehot = (
        (band_row_ids[:, None, None] == jnp.arange(tile_rows, dtype=jnp.int32)[None, :, None])
        & (band_col_ids[:, None, None] == jnp.arange(col_tiles, dtype=jnp.int32)[None, None, :])
    ).astype(jnp.bfloat16)
    band_dense = (
        jnp.einsum("krc,kab->racb", band_onehot, band_tiles, preferred_element_type=jnp.float32)
        .astype(jnp.bfloat16)
        .reshape(row_count, ext_count)
    )
    extended = padded_2(hidden, (("row", 0),), BW)
    band_mixed = jnp.dot(band_dense, extended, preferred_element_type=jnp.float32)
    giving = send_lists[0]
    tile_range = jnp.arange(tile_rows, dtype=jnp.int32)
    send_rows = jnp.where(
        giving[:, None] >= 0,
        giving[:, None] * tile_size + jnp.arange(tile_size, dtype=jnp.int32)[None, :],
        -1,
    ).reshape(peers * tile_size)
    send_pick = (send_rows[:, None] == node_range[None, :]).astype(jnp.bfloat16)
    outgoing = (
        jnp.dot(send_pick, hidden, preferred_element_type=jnp.float32)
        .astype(jnp.bfloat16)
        .reshape(peers, tile_size, width_feat)
    )
    arrived = lax.all_to_all(outgoing, "col", split_axis=0, concat_axis=0, tiled=True)
    owner_range = jnp.arange(peers, dtype=jnp.int32)
    live_slots = jnp.arange(slot_total, dtype=jnp.int32) < bound_count[0]
    bound_row_ids = bound_coords[:, 0]
    bound_owner = bound_coords[:, 1]
    slot_onehot = (
        (bound_row_ids[:, None, None] == tile_range[None, :, None])
        & (bound_owner[:, None, None] == owner_range[None, None, :])
        & live_slots[:, None, None]
    ).astype(jnp.bfloat16)
    bound_dense = jnp.einsum(
        "krs,kab->rasb", slot_onehot, bound_tiles, preferred_element_type=jnp.float32
    ).reshape(row_count, peers * tile_size)
    dense_high = bound_dense.astype(jnp.bfloat16)
    dense_low = (bound_dense - dense_high.astype(jnp.float32)).astype(jnp.bfloat16)
    band_mixed, arrived = lax.optimization_barrier((band_mixed, arrived))
    arrived_rows = arrived.reshape(peers * tile_size, width_feat)
    mixed = band_mixed + jnp.dot(dense_high, arrived_rows, preferred_element_type=jnp.float32)
    mixed = mixed + jnp.dot(dense_low, arrived_rows, preferred_element_type=jnp.float32)
    out_band = jax.nn.silu(mixed).astype(jnp.bfloat16)
    node_out = lax.dot_general(
        band_perm, out_band, contract_rows, preferred_element_type=jnp.float32
    ).astype(jnp.bfloat16)
    grad_band = jnp.dot(band_perm, cotangent, preferred_element_type=jnp.float32)
    sigma = jax.nn.sigmoid(mixed)
    slope = (grad_band * sigma * (1.0 + mixed * (1.0 - sigma))).astype(jnp.bfloat16)
    ext_grad = lax.dot_general(
        band_dense, slope, (((0,), (0,)), ((), ())), preferred_element_type=jnp.float32
    )
    rim_terms = jnp.concatenate([ext_grad[:BW], ext_grad[BW + row_count :]], axis=0).astype(
        jnp.bfloat16
    )
    padded = padded_2(rim_terms, (("row", 0),), BW)
    grad_hidden = ext_grad[BW : BW + row_count]
    grad_hidden = grad_hidden.at[:BW].add(padded[:BW].astype(jnp.float32))
    grad_hidden = grad_hidden.at[row_count - BW :].add(padded[3 * BW :].astype(jnp.float32))
    owner_terms = lax.dot_general(
        dense_high, slope, contract_rows, preferred_element_type=jnp.float32
    ) + lax.dot_general(dense_low, slope, contract_rows, preferred_element_type=jnp.float32)
    to_owner = owner_terms.astype(jnp.bfloat16).reshape(peers, tile_size, width_feat)
    returned = lax.all_to_all(to_owner, "col", split_axis=0, concat_axis=0, tiled=True)
    block_onehot = (giving[None, :] == tile_range[:, None]).astype(jnp.bfloat16)
    from_peers = jnp.einsum(
        "bs,saf->baf", block_onehot, returned, preferred_element_type=jnp.float32
    )
    grad_hidden = grad_hidden + from_peers.reshape(row_count, width_feat)
    grad_round = grad_hidden.astype(jnp.bfloat16)
    partial_weight = lax.dot_general(
        x_band, grad_round, (((0,), (0,)), ((), ())), preferred_element_type=jnp.float32
    )
    nodes_all = row_count * lax.axis_size("row") * peers
    weight_grad = spread_sum(partial_weight, ("row", "col"), nodes_all ** (-0.5))
    feat_band = lax.dot_general(
        grad_round, weight, (((1,), (1,)), ((), ())), preferred_element_type=jnp.float32
    ).astype(jnp.bfloat16)
    feat_grad = lax.dot_general(
        band_perm, feat_band, contract_rows, preferred_element_type=jnp.float32
    ).astype(jnp.bfloat16)
    return (node_out, feat_grad, weight_grad)


def solution(mesh):
    in_specs = (
        P(("row", "col"), None),
        P(),
        P(("row", "col"), None),
        P(("row", "col"), None, None),
        P(("row", "col"), None),
        P(("row", "col"), None, None),
        P(("row", "col"), None),
        P(("row", "col")),
        P(("row", "col"), None),
        P(("row", "col"), None),
        P(("row", "col"), None),
    )
    out_specs = (P(("row", "col"), None), P(("row", "col"), None), P())
    return jax.shard_map(
        on_device, mesh=mesh, in_specs=in_specs, out_specs=out_specs, check_vma=False
    )
```

```python
import jax
import jax.numpy as jnp
from jax import lax
from jax.sharding import PartitionSpec as P

BW = 256


def padded_2(cells, sides, width):
    for axis, dim in sides:
        count = lax.axis_size(axis)
        head = lax.slice_in_dim(cells, 0, width, axis=dim)
        tail = lax.slice_in_dim(cells, cells.shape[dim] - width, cells.shape[dim], axis=dim)
        cells = jnp.concatenate(
            [
                lax.ppermute(tail, axis, [(i, (i + 1) % count) for i in range(count)]),
                cells,
                lax.ppermute(head, axis, [((i + 1) % count, i) for i in range(count)]),
            ],
            axis=dim,
        )
    return cells


def spread_sum(value, axes, scale):
    count = lax.axis_size(axes)
    if value.shape[0] % count == 0:
        piece = (count, value.shape[0] // count, value.shape[1])
    else:
        piece = (count, value.size // count // 128, 128)
    gathered = lax.all_to_all(value.reshape(piece), axes, 0, 0, tiled=True)
    owned = (jnp.sum(gathered, axis=0, keepdims=True) * scale).astype(jnp.bfloat16)
    copies = jnp.broadcast_to(owned, piece)
    spread = lax.all_to_all(copies, axes, 0, 0, tiled=True)
    return spread.astype(jnp.float32).reshape(value.shape)


def on_device(
    node_feats,
    weight,
    cotangent,
    band_tiles,
    band_coords,
    bound_tiles,
    bound_coords,
    bound_count,
    recv_lists,
    send_lists,
    reorder,
):
    tile_size = band_tiles.shape[1]
    row_count = node_feats.shape[0]
    width_feat = node_feats.shape[1]
    tile_rows = row_count // tile_size
    rim_tiles = BW // tile_size
    col_tiles = tile_rows + 2 * rim_tiles
    ext_count = row_count + 2 * BW
    peers = lax.axis_size("col")
    slot_total = bound_tiles.shape[0]
    order = reorder[0]
    node_range = jnp.arange(row_count, dtype=jnp.int32)
    band_perm = (order[:, None] == node_range[None, :]).astype(jnp.bfloat16)
    contract_rows = (((0,), (0,)), ((), ()))
    x_band = jnp.dot(band_perm, node_feats, preferred_element_type=jnp.float32).astype(
        jnp.bfloat16
    )
    hidden = jnp.dot(x_band, weight, preferred_element_type=jnp.float32).astype(jnp.bfloat16)
    band_row_ids = band_coords[:, 0]
    band_col_ids = band_coords[:, 1]
    band_onehot = (
        (band_row_ids[:, None, None] == jnp.arange(tile_rows, dtype=jnp.int32)[None, :, None])
        & (band_col_ids[:, None, None] == jnp.arange(col_tiles, dtype=jnp.int32)[None, None, :])
    ).astype(jnp.bfloat16)
    band_dense = (
        jnp.einsum("krc,kab->racb", band_onehot, band_tiles, preferred_element_type=jnp.float32)
        .astype(jnp.bfloat16)
        .reshape(row_count, ext_count)
    )
    extended = padded_2(hidden, (("row", 0),), BW)
    mixed = jnp.dot(band_dense, extended, preferred_element_type=jnp.float32)
    blocks = hidden.reshape(tile_rows, tile_size, width_feat)
    giving = send_lists[0]
    tile_range = jnp.arange(tile_rows, dtype=jnp.int32)
    give_onehot = (giving[:, None] == tile_range[None, :]).astype(jnp.bfloat16)
    outgoing = jnp.einsum(
        "sb,baf->saf", give_onehot, blocks, preferred_element_type=jnp.float32
    ).astype(jnp.bfloat16)
    arrived = lax.all_to_all(outgoing, "col", split_axis=0, concat_axis=0, tiled=True)
    owner_range = jnp.arange(peers, dtype=jnp.int32)
    live_slots = jnp.arange(slot_total, dtype=jnp.int32) < bound_count[0]
    bound_row_ids = bound_coords[:, 0]
    bound_owner = bound_coords[:, 1]
    slot_onehot = (
        (bound_row_ids[:, None, None] == tile_range[None, :, None])
        & (bound_owner[:, None, None] == owner_range[None, None, :])
        & live_slots[:, None, None]
    ).astype(jnp.bfloat16)
    bound_dense = jnp.einsum(
        "krs,kab->rasb", slot_onehot, bound_tiles, preferred_element_type=jnp.float32
    ).reshape(row_count, peers * tile_size)
    dense_high = bound_dense.astype(jnp.bfloat16)
    dense_low = (bound_dense - dense_high.astype(jnp.float32)).astype(jnp.bfloat16)
    arrived_rows = arrived.reshape(peers * tile_size, width_feat)
    mixed = mixed + jnp.dot(dense_high, arrived_rows, preferred_element_type=jnp.float32)
    mixed = mixed + jnp.dot(dense_low, arrived_rows, preferred_element_type=jnp.float32)
    out_band = jax.nn.silu(mixed).astype(jnp.bfloat16)
    node_out = lax.dot_general(
        band_perm, out_band, contract_rows, preferred_element_type=jnp.float32
    ).astype(jnp.bfloat16)
    grad_band = jnp.dot(band_perm, cotangent, preferred_element_type=jnp.float32)
    sigma = jax.nn.sigmoid(mixed)
    slope = (grad_band * sigma * (1.0 + mixed * (1.0 - sigma))).astype(jnp.bfloat16)
    ext_grad = lax.dot_general(
        band_dense, slope, (((0,), (0,)), ((), ())), preferred_element_type=jnp.float32
    )
    rim_terms = jnp.concatenate([ext_grad[:BW], ext_grad[BW + row_count :]], axis=0).astype(
        jnp.bfloat16
    )
    padded = padded_2(rim_terms, (("row", 0),), BW)
    grad_hidden = ext_grad[BW : BW + row_count]
    grad_hidden = grad_hidden.at[:BW].add(padded[:BW].astype(jnp.float32))
    grad_hidden = grad_hidden.at[row_count - BW :].add(padded[3 * BW :].astype(jnp.float32))
    owner_terms = lax.dot_general(
        jnp.concatenate([dense_high, dense_low], axis=0),
        jnp.concatenate([slope, slope], axis=0),
        contract_rows,
        preferred_element_type=jnp.float32,
    )
    to_owner = owner_terms.astype(jnp.bfloat16).reshape(peers, tile_size, width_feat)
    returned = lax.all_to_all(to_owner, "col", split_axis=0, concat_axis=0, tiled=True)
    block_onehot = (giving[None, :] == tile_range[:, None]).astype(jnp.bfloat16)
    from_peers = jnp.einsum(
        "bs,saf->baf", block_onehot, returned, preferred_element_type=jnp.float32
    )
    grad_hidden = grad_hidden + from_peers.reshape(row_count, width_feat)
    grad_round = grad_hidden.astype(jnp.bfloat16)
    partial_weight = lax.dot_general(
        x_band, grad_round, (((0,), (0,)), ((), ())), preferred_element_type=jnp.float32
    )
    nodes_all = row_count * lax.axis_size("row") * peers
    weight_grad = spread_sum(partial_weight, ("row", "col"), nodes_all ** (-0.5))
    feat_band = lax.dot_general(
        grad_round, weight, (((1,), (1,)), ((), ())), preferred_element_type=jnp.float32
    ).astype(jnp.bfloat16)
    feat_grad = lax.dot_general(
        band_perm, feat_band, contract_rows, preferred_element_type=jnp.float32
    ).astype(jnp.bfloat16)
    return (node_out, feat_grad, weight_grad)


def solution(mesh):
    in_specs = (
        P(("row", "col"), None),
        P(),
        P(("row", "col"), None),
        P(("row", "col"), None, None),
        P(("row", "col"), None),
        P(("row", "col"), None, None),
        P(("row", "col"), None),
        P(("row", "col")),
        P(("row", "col"), None),
        P(("row", "col"), None),
        P(("row", "col"), None),
    )
    out_specs = (P(("row", "col"), None), P(("row", "col"), None), P())
    return jax.shard_map(
        on_device, mesh=mesh, in_specs=in_specs, out_specs=out_specs, check_vma=False
    )
```

```python
import jax
import jax.numpy as jnp
from jax import lax
from jax.sharding import PartitionSpec as P

BW = 256


def padded_2(cells, sides, width):
    for axis, dim in sides:
        count = lax.axis_size(axis)
        head = lax.slice_in_dim(cells, 0, width, axis=dim)
        tail = lax.slice_in_dim(cells, cells.shape[dim] - width, cells.shape[dim], axis=dim)
        cells = jnp.concatenate(
            [
                lax.ppermute(tail, axis, [(i, (i + 1) % count) for i in range(count)]),
                cells,
                lax.ppermute(head, axis, [((i + 1) % count, i) for i in range(count)]),
            ],
            axis=dim,
        )
    return cells


def spread_sum(value, axes, scale):
    count = lax.axis_size(axes)
    if value.shape[0] % count == 0:
        piece = (count, value.shape[0] // count, value.shape[1])
    else:
        piece = (count, value.size // count // 128, 128)
    gathered = lax.all_to_all(value.reshape(piece), axes, 0, 0, tiled=True)
    owned = (jnp.sum(gathered, axis=0, keepdims=True) * scale).astype(jnp.bfloat16)
    copies = jnp.broadcast_to(owned, piece)
    spread = lax.all_to_all(copies, axes, 0, 0, tiled=True)
    return spread.astype(jnp.float32).reshape(value.shape)


def on_device(
    node_feats,
    weight,
    cotangent,
    band_tiles,
    band_coords,
    bound_tiles,
    bound_coords,
    bound_count,
    recv_lists,
    send_lists,
    reorder,
):
    tile_size = band_tiles.shape[1]
    row_count = node_feats.shape[0]
    width_feat = node_feats.shape[1]
    tile_rows = row_count // tile_size
    rim_tiles = BW // tile_size
    col_tiles = tile_rows + 2 * rim_tiles
    ext_count = row_count + 2 * BW
    peers = lax.axis_size("col")
    slot_total = bound_tiles.shape[0]
    order = reorder[0]
    node_range = jnp.arange(row_count, dtype=jnp.int32)
    band_perm = (order[:, None] == node_range[None, :]).astype(jnp.bfloat16)
    contract_rows = (((0,), (0,)), ((), ()))
    x_band = jnp.dot(band_perm, node_feats, preferred_element_type=jnp.float32).astype(
        jnp.bfloat16
    )
    hidden = jnp.dot(x_band, weight, preferred_element_type=jnp.float32).astype(jnp.bfloat16)
    band_row_ids = band_coords[:, 0]
    band_col_ids = band_coords[:, 1]
    band_onehot = (
        (band_row_ids[:, None, None] == jnp.arange(tile_rows, dtype=jnp.int32)[None, :, None])
        & (band_col_ids[:, None, None] == jnp.arange(col_tiles, dtype=jnp.int32)[None, None, :])
    ).astype(jnp.bfloat16)
    band_dense = (
        jnp.einsum("krc,kab->racb", band_onehot, band_tiles, preferred_element_type=jnp.float32)
        .astype(jnp.bfloat16)
        .reshape(row_count, ext_count)
    )
    extended = padded_2(hidden, (("row", 0),), BW)
    mixed = jnp.dot(band_dense, extended, preferred_element_type=jnp.float32)
    blocks = hidden.reshape(tile_rows, tile_size, width_feat)
    giving = send_lists[0]
    tile_range = jnp.arange(tile_rows, dtype=jnp.int32)
    give_onehot = (giving[:, None] == tile_range[None, :]).astype(jnp.bfloat16)
    outgoing = jnp.einsum(
        "sb,baf->saf", give_onehot, blocks, preferred_element_type=jnp.float32
    ).astype(jnp.bfloat16)
    arrived = lax.all_to_all(outgoing, "col", split_axis=0, concat_axis=0, tiled=True)
    owner_range = jnp.arange(peers, dtype=jnp.int32)
    live_slots = jnp.arange(slot_total, dtype=jnp.int32) < bound_count[0]
    bound_row_ids = bound_coords[:, 0]
    bound_owner = bound_coords[:, 1]
    slot_onehot = (
        (bound_row_ids[:, None, None] == tile_range[None, :, None])
        & (bound_owner[:, None, None] == owner_range[None, None, :])
        & live_slots[:, None, None]
    ).astype(jnp.bfloat16)
    bound_dense = jnp.einsum(
        "krs,kab->rasb", slot_onehot, bound_tiles, preferred_element_type=jnp.float32
    ).reshape(row_count, peers * tile_size)
    dense_high = bound_dense.astype(jnp.bfloat16)
    dense_low = (bound_dense - dense_high.astype(jnp.float32)).astype(jnp.bfloat16)
    arrived_rows = arrived.reshape(peers * tile_size, width_feat)
    mixed = mixed + jnp.dot(
        jnp.concatenate([dense_high, dense_low], axis=1),
        jnp.concatenate([arrived_rows, arrived_rows], axis=0),
        preferred_element_type=jnp.float32,
    )
    out_band = jax.nn.silu(mixed).astype(jnp.bfloat16)
    node_out = lax.dot_general(
        band_perm, out_band, contract_rows, preferred_element_type=jnp.float32
    ).astype(jnp.bfloat16)
    grad_band = jnp.dot(band_perm, cotangent, preferred_element_type=jnp.float32)
    sigma = jax.nn.sigmoid(mixed)
    slope = (grad_band * sigma * (1.0 + mixed * (1.0 - sigma))).astype(jnp.bfloat16)
    ext_grad = lax.dot_general(
        band_dense, slope, (((0,), (0,)), ((), ())), preferred_element_type=jnp.float32
    )
    rim_terms = jnp.concatenate([ext_grad[:BW], ext_grad[BW + row_count :]], axis=0).astype(
        jnp.bfloat16
    )
    padded = padded_2(rim_terms, (("row", 0),), BW)
    grad_hidden = ext_grad[BW : BW + row_count]
    grad_hidden = grad_hidden.at[:BW].add(padded[:BW].astype(jnp.float32))
    grad_hidden = grad_hidden.at[row_count - BW :].add(padded[3 * BW :].astype(jnp.float32))
    owner_terms = lax.dot_general(
        jnp.concatenate([dense_high, dense_low], axis=0),
        jnp.concatenate([slope, slope], axis=0),
        contract_rows,
        preferred_element_type=jnp.float32,
    )
    to_owner = owner_terms.astype(jnp.bfloat16).reshape(peers, tile_size, width_feat)
    returned = lax.all_to_all(to_owner, "col", split_axis=0, concat_axis=0, tiled=True)
    block_onehot = (giving[None, :] == tile_range[:, None]).astype(jnp.bfloat16)
    from_peers = jnp.einsum(
        "bs,saf->baf", block_onehot, returned, preferred_element_type=jnp.float32
    )
    grad_hidden = grad_hidden + from_peers.reshape(row_count, width_feat)
    grad_round = grad_hidden.astype(jnp.bfloat16)
    partial_weight = lax.dot_general(
        x_band, grad_round, (((0,), (0,)), ((), ())), preferred_element_type=jnp.float32
    )
    nodes_all = row_count * lax.axis_size("row") * peers
    weight_grad = spread_sum(partial_weight, ("row", "col"), nodes_all ** (-0.5))
    feat_band = lax.dot_general(
        grad_round, weight, (((1,), (1,)), ((), ())), preferred_element_type=jnp.float32
    ).astype(jnp.bfloat16)
    feat_grad = lax.dot_general(
        band_perm, feat_band, contract_rows, preferred_element_type=jnp.float32
    ).astype(jnp.bfloat16)
    return (node_out, feat_grad, weight_grad)


def solution(mesh):
    in_specs = (
        P(("row", "col"), None),
        P(),
        P(("row", "col"), None),
        P(("row", "col"), None, None),
        P(("row", "col"), None),
        P(("row", "col"), None, None),
        P(("row", "col"), None),
        P(("row", "col")),
        P(("row", "col"), None),
        P(("row", "col"), None),
        P(("row", "col"), None),
    )
    out_specs = (P(("row", "col"), None), P(("row", "col"), None), P())
    return jax.shard_map(
        on_device, mesh=mesh, in_specs=in_specs, out_specs=out_specs, check_vma=False
    )
```

```python
import jax
import jax.numpy as jnp
from jax import lax
from jax.sharding import PartitionSpec as P

BW = 256


def padded_2(cells, sides, width):
    for axis, dim in sides:
        count = lax.axis_size(axis)
        head = lax.slice_in_dim(cells, 0, width, axis=dim)
        tail = lax.slice_in_dim(cells, cells.shape[dim] - width, cells.shape[dim], axis=dim)
        cells = jnp.concatenate(
            [
                lax.ppermute(tail, axis, [(i, (i + 1) % count) for i in range(count)]),
                cells,
                lax.ppermute(head, axis, [((i + 1) % count, i) for i in range(count)]),
            ],
            axis=dim,
        )
    return cells


def spread_sum(value, axes, scale):
    count = lax.axis_size(axes)
    if value.shape[0] % count == 0:
        piece = (count, value.shape[0] // count, value.shape[1])
    else:
        piece = (count, value.size // count // 128, 128)
    gathered = lax.all_to_all(value.reshape(piece), axes, 0, 0, tiled=True)
    owned = (jnp.sum(gathered, axis=0, keepdims=True) * scale).astype(jnp.bfloat16)
    copies = jnp.broadcast_to(owned, piece)
    spread = lax.all_to_all(copies, axes, 0, 0, tiled=True)
    return spread.astype(jnp.float32).reshape(value.shape)


def on_device(
    node_feats,
    weight,
    cotangent,
    band_tiles,
    band_coords,
    bound_tiles,
    bound_coords,
    bound_count,
    recv_lists,
    send_lists,
    reorder,
):
    tile_size = band_tiles.shape[1]
    row_count = node_feats.shape[0]
    width_feat = node_feats.shape[1]
    tile_rows = row_count // tile_size
    rim_tiles = BW // tile_size
    col_tiles = tile_rows + 2 * rim_tiles
    ext_count = row_count + 2 * BW
    peers = lax.axis_size("col")
    slot_total = bound_tiles.shape[0]
    order = reorder[0]
    node_range = jnp.arange(row_count, dtype=jnp.int32)
    band_perm = (order[:, None] == node_range[None, :]).astype(jnp.bfloat16)
    contract_rows = (((0,), (0,)), ((), ()))
    x_band = jnp.dot(band_perm, node_feats, preferred_element_type=jnp.float32).astype(
        jnp.bfloat16
    )
    hidden = jnp.dot(x_band, weight, preferred_element_type=jnp.float32).astype(jnp.bfloat16)
    band_row_ids = band_coords[:, 0]
    band_col_ids = band_coords[:, 1]
    band_onehot = (
        (band_row_ids[:, None, None] == jnp.arange(tile_rows, dtype=jnp.int32)[None, :, None])
        & (band_col_ids[:, None, None] == jnp.arange(col_tiles, dtype=jnp.int32)[None, None, :])
    ).astype(jnp.bfloat16)
    band_dense = (
        jnp.einsum("krc,kab->racb", band_onehot, band_tiles, preferred_element_type=jnp.float32)
        .astype(jnp.bfloat16)
        .reshape(row_count, ext_count)
    )
    extended = padded_2(hidden, (("row", 0),), BW)
    blocks = hidden.reshape(tile_rows, tile_size, width_feat)
    giving = send_lists[0]
    tile_range = jnp.arange(tile_rows, dtype=jnp.int32)
    give_onehot = (giving[:, None] == tile_range[None, :]).astype(jnp.bfloat16)
    outgoing = jnp.einsum(
        "sb,baf->saf", give_onehot, blocks, preferred_element_type=jnp.float32
    ).astype(jnp.bfloat16)
    arrived = lax.all_to_all(outgoing, "col", split_axis=0, concat_axis=0, tiled=True)
    owner_range = jnp.arange(peers, dtype=jnp.int32)
    live_slots = jnp.arange(slot_total, dtype=jnp.int32) < bound_count[0]
    bound_row_ids = bound_coords[:, 0]
    bound_owner = bound_coords[:, 1]
    slot_onehot = (
        (bound_row_ids[:, None, None] == tile_range[None, :, None])
        & (bound_owner[:, None, None] == owner_range[None, None, :])
        & live_slots[:, None, None]
    ).astype(jnp.bfloat16)
    bound_dense = jnp.einsum(
        "krs,kab->rasb", slot_onehot, bound_tiles, preferred_element_type=jnp.float32
    ).reshape(row_count, peers * tile_size)
    dense_high = bound_dense.astype(jnp.bfloat16)
    dense_low = (bound_dense - dense_high.astype(jnp.float32)).astype(jnp.bfloat16)
    arrived_rows = arrived.reshape(peers * tile_size, width_feat)
    mixed = jnp.dot(
        jnp.concatenate([band_dense, dense_high, dense_low], axis=1),
        jnp.concatenate([extended, arrived_rows, arrived_rows], axis=0),
        preferred_element_type=jnp.float32,
    )
    out_band = jax.nn.silu(mixed).astype(jnp.bfloat16)
    node_out = lax.dot_general(
        band_perm, out_band, contract_rows, preferred_element_type=jnp.float32
    ).astype(jnp.bfloat16)
    grad_band = jnp.dot(band_perm, cotangent, preferred_element_type=jnp.float32)
    sigma = jax.nn.sigmoid(mixed)
    slope = (grad_band * sigma * (1.0 + mixed * (1.0 - sigma))).astype(jnp.bfloat16)
    ext_grad = lax.dot_general(
        band_dense, slope, (((0,), (0,)), ((), ())), preferred_element_type=jnp.float32
    )
    rim_terms = jnp.concatenate([ext_grad[:BW], ext_grad[BW + row_count :]], axis=0).astype(
        jnp.bfloat16
    )
    padded = padded_2(rim_terms, (("row", 0),), BW)
    grad_hidden = ext_grad[BW : BW + row_count]
    grad_hidden = grad_hidden.at[:BW].add(padded[:BW].astype(jnp.float32))
    grad_hidden = grad_hidden.at[row_count - BW :].add(padded[3 * BW :].astype(jnp.float32))
    owner_terms = lax.dot_general(
        jnp.concatenate([dense_high, dense_low], axis=0),
        jnp.concatenate([slope, slope], axis=0),
        contract_rows,
        preferred_element_type=jnp.float32,
    )
    to_owner = owner_terms.astype(jnp.bfloat16).reshape(peers, tile_size, width_feat)
    returned = lax.all_to_all(to_owner, "col", split_axis=0, concat_axis=0, tiled=True)
    block_onehot = (giving[None, :] == tile_range[:, None]).astype(jnp.bfloat16)
    from_peers = jnp.einsum(
        "bs,saf->baf", block_onehot, returned, preferred_element_type=jnp.float32
    )
    grad_hidden = grad_hidden + from_peers.reshape(row_count, width_feat)
    grad_round = grad_hidden.astype(jnp.bfloat16)
    partial_weight = lax.dot_general(
        x_band, grad_round, (((0,), (0,)), ((), ())), preferred_element_type=jnp.float32
    )
    nodes_all = row_count * lax.axis_size("row") * peers
    weight_grad = spread_sum(partial_weight, ("row", "col"), nodes_all ** (-0.5))
    feat_band = lax.dot_general(
        grad_round, weight, (((1,), (1,)), ((), ())), preferred_element_type=jnp.float32
    ).astype(jnp.bfloat16)
    feat_grad = lax.dot_general(
        band_perm, feat_band, contract_rows, preferred_element_type=jnp.float32
    ).astype(jnp.bfloat16)
    return (node_out, feat_grad, weight_grad)


def solution(mesh):
    in_specs = (
        P(("row", "col"), None),
        P(),
        P(("row", "col"), None),
        P(("row", "col"), None, None),
        P(("row", "col"), None),
        P(("row", "col"), None, None),
        P(("row", "col"), None),
        P(("row", "col")),
        P(("row", "col"), None),
        P(("row", "col"), None),
        P(("row", "col"), None),
    )
    out_specs = (P(("row", "col"), None), P(("row", "col"), None), P())
    return jax.shard_map(
        on_device, mesh=mesh, in_specs=in_specs, out_specs=out_specs, check_vma=False
    )
```

```python
import jax
import jax.numpy as jnp
from jax import lax
from jax.sharding import PartitionSpec as P

BW = 256


def padded_2(cells, sides, width):
    for axis, dim in sides:
        count = lax.axis_size(axis)
        head = lax.slice_in_dim(cells, 0, width, axis=dim)
        tail = lax.slice_in_dim(cells, cells.shape[dim] - width, cells.shape[dim], axis=dim)
        cells = jnp.concatenate(
            [
                lax.ppermute(tail, axis, [(i, (i + 1) % count) for i in range(count)]),
                cells,
                lax.ppermute(head, axis, [((i + 1) % count, i) for i in range(count)]),
            ],
            axis=dim,
        )
    return cells


def spread_sum(value, axes, scale):
    count = lax.axis_size(axes)
    if value.shape[0] % count == 0:
        piece = (count, value.shape[0] // count, value.shape[1])
    else:
        piece = (count, value.size // count // 128, 128)
    gathered = lax.all_to_all(value.reshape(piece), axes, 0, 0, tiled=True)
    owned = (jnp.sum(gathered, axis=0, keepdims=True) * scale).astype(jnp.bfloat16)
    copies = jnp.broadcast_to(owned, piece)
    spread = lax.all_to_all(copies, axes, 0, 0, tiled=True)
    return spread.astype(jnp.float32).reshape(value.shape)


def on_device(
    node_feats,
    weight,
    cotangent,
    band_tiles,
    band_coords,
    bound_tiles,
    bound_coords,
    bound_count,
    recv_lists,
    send_lists,
    reorder,
):
    tile_size = band_tiles.shape[1]
    row_count = node_feats.shape[0]
    width_feat = node_feats.shape[1]
    tile_rows = row_count // tile_size
    rim_tiles = BW // tile_size
    col_tiles = tile_rows + 2 * rim_tiles
    ext_count = row_count + 2 * BW
    peers = lax.axis_size("col")
    slot_total = bound_tiles.shape[0]
    order = reorder[0]
    node_range = jnp.arange(row_count, dtype=jnp.int32)
    band_perm = (order[:, None] == node_range[None, :]).astype(jnp.bfloat16)
    contract_rows = (((0,), (0,)), ((), ()))
    x_band = jnp.dot(band_perm, node_feats, preferred_element_type=jnp.float32).astype(
        jnp.bfloat16
    )
    hidden = jnp.dot(x_band, weight, preferred_element_type=jnp.float32).astype(jnp.bfloat16)
    band_row_ids = band_coords[:, 0]
    band_col_ids = band_coords[:, 1]
    band_onehot = (
        (band_row_ids[:, None, None] == jnp.arange(tile_rows, dtype=jnp.int32)[None, :, None])
        & (band_col_ids[:, None, None] == jnp.arange(col_tiles, dtype=jnp.int32)[None, None, :])
    ).astype(jnp.bfloat16)
    band_dense = (
        jnp.einsum("krc,kab->racb", band_onehot, band_tiles, preferred_element_type=jnp.float32)
        .astype(jnp.bfloat16)
        .reshape(row_count, ext_count)
    )
    extended = padded_2(hidden, (("row", 0),), BW)
    band_mixed = jnp.dot(band_dense, extended, preferred_element_type=jnp.float32)
    blocks = hidden.reshape(tile_rows, tile_size, width_feat)
    giving = send_lists[0]
    tile_range = jnp.arange(tile_rows, dtype=jnp.int32)
    give_onehot = (giving[:, None] == tile_range[None, :]).astype(jnp.bfloat16)
    outgoing = jnp.einsum(
        "sb,baf->saf", give_onehot, blocks, preferred_element_type=jnp.float32
    ).astype(jnp.bfloat16)
    arrived = lax.all_to_all(outgoing, "col", split_axis=0, concat_axis=0, tiled=True)
    owner_range = jnp.arange(peers, dtype=jnp.int32)
    live_slots = jnp.arange(slot_total, dtype=jnp.int32) < bound_count[0]
    bound_row_ids = bound_coords[:, 0]
    bound_owner = bound_coords[:, 1]
    slot_onehot = (
        (bound_row_ids[:, None, None] == tile_range[None, :, None])
        & (bound_owner[:, None, None] == owner_range[None, None, :])
        & live_slots[:, None, None]
    ).astype(jnp.bfloat16)
    bound_dense = jnp.einsum(
        "krs,kab->rasb", slot_onehot, bound_tiles, preferred_element_type=jnp.float32
    ).reshape(row_count, peers * tile_size)
    dense_high = bound_dense.astype(jnp.bfloat16)
    dense_low = (bound_dense - dense_high.astype(jnp.float32)).astype(jnp.bfloat16)
    band_mixed, arrived = lax.optimization_barrier((band_mixed, arrived))
    arrived_rows = arrived.reshape(peers * tile_size, width_feat)
    mixed = band_mixed + jnp.dot(
        jnp.concatenate([dense_high, dense_low], axis=1),
        jnp.concatenate([arrived_rows, arrived_rows], axis=0),
        preferred_element_type=jnp.float32,
    )
    out_band = jax.nn.silu(mixed).astype(jnp.bfloat16)
    node_out = lax.dot_general(
        band_perm, out_band, contract_rows, preferred_element_type=jnp.float32
    ).astype(jnp.bfloat16)
    grad_band = jnp.dot(band_perm, cotangent, preferred_element_type=jnp.float32)
    sigma = jax.nn.sigmoid(mixed)
    slope = (grad_band * sigma * (1.0 + mixed * (1.0 - sigma))).astype(jnp.bfloat16)
    ext_grad = lax.dot_general(
        band_dense, slope, (((0,), (0,)), ((), ())), preferred_element_type=jnp.float32
    )
    rim_terms = jnp.concatenate([ext_grad[:BW], ext_grad[BW + row_count :]], axis=0).astype(
        jnp.bfloat16
    )
    padded = padded_2(rim_terms, (("row", 0),), BW)
    grad_hidden = ext_grad[BW : BW + row_count]
    grad_hidden = grad_hidden.at[:BW].add(padded[:BW].astype(jnp.float32))
    grad_hidden = grad_hidden.at[row_count - BW :].add(padded[3 * BW :].astype(jnp.float32))
    owner_terms = lax.dot_general(
        jnp.concatenate([dense_high, dense_low], axis=0),
        jnp.concatenate([slope, slope], axis=0),
        contract_rows,
        preferred_element_type=jnp.float32,
    )
    to_owner = owner_terms.astype(jnp.bfloat16).reshape(peers, tile_size, width_feat)
    returned = lax.all_to_all(to_owner, "col", split_axis=0, concat_axis=0, tiled=True)
    block_onehot = (giving[None, :] == tile_range[:, None]).astype(jnp.bfloat16)
    from_peers = jnp.einsum(
        "bs,saf->baf", block_onehot, returned, preferred_element_type=jnp.float32
    )
    grad_hidden = grad_hidden + from_peers.reshape(row_count, width_feat)
    grad_round = grad_hidden.astype(jnp.bfloat16)
    partial_weight = lax.dot_general(
        x_band, grad_round, (((0,), (0,)), ((), ())), preferred_element_type=jnp.float32
    )
    nodes_all = row_count * lax.axis_size("row") * peers
    weight_grad = spread_sum(partial_weight, ("row", "col"), nodes_all ** (-0.5))
    feat_band = lax.dot_general(
        grad_round, weight, (((1,), (1,)), ((), ())), preferred_element_type=jnp.float32
    ).astype(jnp.bfloat16)
    feat_grad = lax.dot_general(
        band_perm, feat_band, contract_rows, preferred_element_type=jnp.float32
    ).astype(jnp.bfloat16)
    return (node_out, feat_grad, weight_grad)


def solution(mesh):
    in_specs = (
        P(("row", "col"), None),
        P(),
        P(("row", "col"), None),
        P(("row", "col"), None, None),
        P(("row", "col"), None),
        P(("row", "col"), None, None),
        P(("row", "col"), None),
        P(("row", "col")),
        P(("row", "col"), None),
        P(("row", "col"), None),
        P(("row", "col"), None),
    )
    out_specs = (P(("row", "col"), None), P(("row", "col"), None), P())
    return jax.shard_map(
        on_device, mesh=mesh, in_specs=in_specs, out_specs=out_specs, check_vma=False
    )
```

```python
import jax
import jax.numpy as jnp
from jax import lax
from jax.sharding import PartitionSpec as P

BW = 256


def padded_2(cells, sides, width):
    for axis, dim in sides:
        count = lax.axis_size(axis)
        head = lax.slice_in_dim(cells, 0, width, axis=dim)
        tail = lax.slice_in_dim(cells, cells.shape[dim] - width, cells.shape[dim], axis=dim)
        cells = jnp.concatenate(
            [
                lax.ppermute(tail, axis, [(i, (i + 1) % count) for i in range(count)]),
                cells,
                lax.ppermute(head, axis, [((i + 1) % count, i) for i in range(count)]),
            ],
            axis=dim,
        )
    return cells


def spread_sum(value, axes, scale):
    count = lax.axis_size(axes)
    if value.shape[0] % count == 0:
        piece = (count, value.shape[0] // count, value.shape[1])
    else:
        piece = (count, value.size // count // 128, 128)
    gathered = lax.all_to_all(value.reshape(piece), axes, 0, 0, tiled=True)
    owned = (jnp.sum(gathered, axis=0, keepdims=True) * scale).astype(jnp.bfloat16)
    copies = jnp.broadcast_to(owned, piece)
    spread = lax.all_to_all(copies, axes, 0, 0, tiled=True)
    return spread.astype(jnp.float32).reshape(value.shape)


def on_device(
    node_feats,
    weight,
    cotangent,
    band_tiles,
    band_coords,
    bound_tiles,
    bound_coords,
    bound_count,
    recv_lists,
    send_lists,
    reorder,
):
    tile_size = band_tiles.shape[1]
    row_count = node_feats.shape[0]
    width_feat = node_feats.shape[1]
    tile_rows = row_count // tile_size
    rim_tiles = BW // tile_size
    col_tiles = tile_rows + 2 * rim_tiles
    ext_count = row_count + 2 * BW
    peers = lax.axis_size("col")
    slot_total = bound_tiles.shape[0]
    order = reorder[0]
    node_range = jnp.arange(row_count, dtype=jnp.int32)
    band_perm = (order[:, None] == node_range[None, :]).astype(jnp.bfloat16)
    contract_rows = (((0,), (0,)), ((), ()))
    x_band = jnp.dot(band_perm, node_feats, preferred_element_type=jnp.float32).astype(
        jnp.bfloat16
    )
    hidden = jnp.dot(x_band, weight, preferred_element_type=jnp.float32).astype(jnp.bfloat16)
    band_row_ids = band_coords[:, 0]
    band_col_ids = band_coords[:, 1]
    band_onehot = (
        (band_row_ids[:, None, None] == jnp.arange(tile_rows, dtype=jnp.int32)[None, :, None])
        & (band_col_ids[:, None, None] == jnp.arange(col_tiles, dtype=jnp.int32)[None, None, :])
    ).astype(jnp.bfloat16)
    band_dense = (
        jnp.einsum("krc,kab->racb", band_onehot, band_tiles, preferred_element_type=jnp.float32)
        .astype(jnp.bfloat16)
        .reshape(row_count, ext_count)
    )
    extended = padded_2(hidden, (("row", 0),), BW)
    mixed = jnp.dot(band_dense, extended, preferred_element_type=jnp.float32)
    giving = send_lists[0]
    tile_range = jnp.arange(tile_rows, dtype=jnp.int32)
    send_rows = jnp.where(
        giving[:, None] >= 0,
        giving[:, None] * tile_size + jnp.arange(tile_size, dtype=jnp.int32)[None, :],
        -1,
    ).reshape(peers * tile_size)
    send_pick = (send_rows[:, None] == node_range[None, :]).astype(jnp.bfloat16)
    outgoing = (
        jnp.dot(send_pick, hidden, preferred_element_type=jnp.float32)
        .astype(jnp.bfloat16)
        .reshape(peers, tile_size, width_feat)
    )
    arrived = lax.all_to_all(outgoing, "col", split_axis=0, concat_axis=0, tiled=True)
    owner_range = jnp.arange(peers, dtype=jnp.int32)
    live_slots = jnp.arange(slot_total, dtype=jnp.int32) < bound_count[0]
    bound_row_ids = bound_coords[:, 0]
    bound_owner = bound_coords[:, 1]
    slot_onehot = (
        (bound_row_ids[:, None, None] == tile_range[None, :, None])
        & (bound_owner[:, None, None] == owner_range[None, None, :])
        & live_slots[:, None, None]
    ).astype(jnp.bfloat16)
    bound_dense = jnp.einsum(
        "krs,kab->rasb", slot_onehot, bound_tiles, preferred_element_type=jnp.float32
    ).reshape(row_count, peers * tile_size)
    dense_high = bound_dense.astype(jnp.bfloat16)
    dense_low = (bound_dense - dense_high.astype(jnp.float32)).astype(jnp.bfloat16)
    arrived_rows = arrived.reshape(peers * tile_size, width_feat)
    mixed = mixed + jnp.dot(
        jnp.concatenate([dense_high, dense_low], axis=1),
        jnp.concatenate([arrived_rows, arrived_rows], axis=0),
        preferred_element_type=jnp.float32,
    )
    out_band = jax.nn.silu(mixed).astype(jnp.bfloat16)
    node_out = lax.dot_general(
        band_perm, out_band, contract_rows, preferred_element_type=jnp.float32
    ).astype(jnp.bfloat16)
    grad_band = jnp.dot(band_perm, cotangent, preferred_element_type=jnp.float32)
    sigma = jax.nn.sigmoid(mixed)
    slope = (grad_band * sigma * (1.0 + mixed * (1.0 - sigma))).astype(jnp.bfloat16)
    ext_grad = lax.dot_general(
        band_dense, slope, (((0,), (0,)), ((), ())), preferred_element_type=jnp.float32
    )
    rim_terms = jnp.concatenate([ext_grad[:BW], ext_grad[BW + row_count :]], axis=0).astype(
        jnp.bfloat16
    )
    padded = padded_2(rim_terms, (("row", 0),), BW)
    grad_hidden = ext_grad[BW : BW + row_count]
    grad_hidden = grad_hidden.at[:BW].add(padded[:BW].astype(jnp.float32))
    grad_hidden = grad_hidden.at[row_count - BW :].add(padded[3 * BW :].astype(jnp.float32))
    owner_terms = lax.dot_general(
        jnp.concatenate([dense_high, dense_low], axis=0),
        jnp.concatenate([slope, slope], axis=0),
        contract_rows,
        preferred_element_type=jnp.float32,
    )
    to_owner = owner_terms.astype(jnp.bfloat16).reshape(peers, tile_size, width_feat)
    returned = lax.all_to_all(to_owner, "col", split_axis=0, concat_axis=0, tiled=True)
    block_onehot = (giving[None, :] == tile_range[:, None]).astype(jnp.bfloat16)
    from_peers = jnp.einsum(
        "bs,saf->baf", block_onehot, returned, preferred_element_type=jnp.float32
    )
    grad_hidden = grad_hidden + from_peers.reshape(row_count, width_feat)
    grad_round = grad_hidden.astype(jnp.bfloat16)
    partial_weight = lax.dot_general(
        x_band, grad_round, (((0,), (0,)), ((), ())), preferred_element_type=jnp.float32
    )
    nodes_all = row_count * lax.axis_size("row") * peers
    weight_grad = spread_sum(partial_weight, ("row", "col"), nodes_all ** (-0.5))
    feat_band = lax.dot_general(
        grad_round, weight, (((1,), (1,)), ((), ())), preferred_element_type=jnp.float32
    ).astype(jnp.bfloat16)
    feat_grad = lax.dot_general(
        band_perm, feat_band, contract_rows, preferred_element_type=jnp.float32
    ).astype(jnp.bfloat16)
    return (node_out, feat_grad, weight_grad)


def solution(mesh):
    in_specs = (
        P(("row", "col"), None),
        P(),
        P(("row", "col"), None),
        P(("row", "col"), None, None),
        P(("row", "col"), None),
        P(("row", "col"), None, None),
        P(("row", "col"), None),
        P(("row", "col")),
        P(("row", "col"), None),
        P(("row", "col"), None),
        P(("row", "col"), None),
    )
    out_specs = (P(("row", "col"), None), P(("row", "col"), None), P())
    return jax.shard_map(
        on_device, mesh=mesh, in_specs=in_specs, out_specs=out_specs, check_vma=False
    )
```

```python
import jax
import jax.numpy as jnp
from jax import lax
from jax.sharding import PartitionSpec as P

BW = 256


def padded_2(cells, sides, width):
    for axis, dim in sides:
        count = lax.axis_size(axis)
        head = lax.slice_in_dim(cells, 0, width, axis=dim)
        tail = lax.slice_in_dim(cells, cells.shape[dim] - width, cells.shape[dim], axis=dim)
        cells = jnp.concatenate(
            [
                lax.ppermute(tail, axis, [(i, (i + 1) % count) for i in range(count)]),
                cells,
                lax.ppermute(head, axis, [((i + 1) % count, i) for i in range(count)]),
            ],
            axis=dim,
        )
    return cells


def spread_sum(value, axes, scale):
    count = lax.axis_size(axes)
    if value.shape[0] % count == 0:
        piece = (count, value.shape[0] // count, value.shape[1])
    else:
        piece = (count, value.size // count // 128, 128)
    gathered = lax.all_to_all(value.reshape(piece), axes, 0, 0, tiled=True)
    owned = (jnp.sum(gathered, axis=0, keepdims=True) * scale).astype(jnp.bfloat16)
    copies = jnp.broadcast_to(owned, piece)
    spread = lax.all_to_all(copies, axes, 0, 0, tiled=True)
    return spread.astype(jnp.float32).reshape(value.shape)


def on_device(
    node_feats,
    weight,
    cotangent,
    band_tiles,
    band_coords,
    bound_tiles,
    bound_coords,
    bound_count,
    recv_lists,
    send_lists,
    reorder,
):
    tile_size = band_tiles.shape[1]
    row_count = node_feats.shape[0]
    width_feat = node_feats.shape[1]
    tile_rows = row_count // tile_size
    rim_tiles = BW // tile_size
    col_tiles = tile_rows + 2 * rim_tiles
    ext_count = row_count + 2 * BW
    peers = lax.axis_size("col")
    slot_total = bound_tiles.shape[0]
    order = reorder[0]
    node_range = jnp.arange(row_count, dtype=jnp.int32)
    band_perm = (order[:, None] == node_range[None, :]).astype(jnp.bfloat16)
    contract_rows = (((0,), (0,)), ((), ()))
    x_band = jnp.dot(band_perm, node_feats, preferred_element_type=jnp.float32).astype(
        jnp.bfloat16
    )
    hidden = jnp.dot(x_band, weight, preferred_element_type=jnp.float32).astype(jnp.bfloat16)
    band_row_ids = band_coords[:, 0]
    band_col_ids = band_coords[:, 1]
    band_onehot = (
        (band_row_ids[:, None, None] == jnp.arange(tile_rows, dtype=jnp.int32)[None, :, None])
        & (band_col_ids[:, None, None] == jnp.arange(col_tiles, dtype=jnp.int32)[None, None, :])
    ).astype(jnp.bfloat16)
    band_dense = (
        jnp.einsum("krc,kab->racb", band_onehot, band_tiles, preferred_element_type=jnp.float32)
        .astype(jnp.bfloat16)
        .reshape(row_count, ext_count)
    )
    extended = padded_2(hidden, (("row", 0),), BW)
    mixed = jnp.dot(band_dense, extended, preferred_element_type=jnp.float32)
    blocks = hidden.reshape(tile_rows, tile_size, width_feat)
    giving = send_lists[0]
    tile_range = jnp.arange(tile_rows, dtype=jnp.int32)
    give_onehot = (giving[:, None] == tile_range[None, :]).astype(jnp.bfloat16)
    outgoing = jnp.einsum(
        "sb,baf->saf", give_onehot, blocks, preferred_element_type=jnp.float32
    ).astype(jnp.bfloat16)
    arrived = lax.all_to_all(outgoing, "col", split_axis=0, concat_axis=0, tiled=True)
    owner_range = jnp.arange(peers, dtype=jnp.int32)
    live_slots = jnp.arange(slot_total, dtype=jnp.int32) < bound_count[0]
    bound_row_ids = bound_coords[:, 0]
    bound_owner = bound_coords[:, 1]
    slot_onehot = (
        (bound_row_ids[:, None, None] == tile_range[None, :, None])
        & (bound_owner[:, None, None] == owner_range[None, None, :])
        & live_slots[:, None, None]
    ).astype(jnp.bfloat16)
    bound_dense = jnp.einsum(
        "krs,kab->rasb", slot_onehot, bound_tiles, preferred_element_type=jnp.float32
    ).reshape(row_count, peers * tile_size)
    dense_high = bound_dense.astype(jnp.bfloat16)
    dense_low = (bound_dense - dense_high.astype(jnp.float32)).astype(jnp.bfloat16)
    bound_dense_t = jnp.einsum(
        "krs,kab->sbra", slot_onehot, bound_tiles, preferred_element_type=jnp.float32
    ).reshape(peers * tile_size, row_count)
    dense_high_t = bound_dense_t.astype(jnp.bfloat16)
    dense_low_t = (bound_dense_t - dense_high_t.astype(jnp.float32)).astype(jnp.bfloat16)
    arrived_rows = arrived.reshape(peers * tile_size, width_feat)
    mixed = mixed + jnp.dot(
        jnp.concatenate([dense_high, dense_low], axis=1),
        jnp.concatenate([arrived_rows, arrived_rows], axis=0),
        preferred_element_type=jnp.float32,
    )
    out_band = jax.nn.silu(mixed).astype(jnp.bfloat16)
    node_out = lax.dot_general(
        band_perm, out_band, contract_rows, preferred_element_type=jnp.float32
    ).astype(jnp.bfloat16)
    grad_band = jnp.dot(band_perm, cotangent, preferred_element_type=jnp.float32)
    sigma = jax.nn.sigmoid(mixed)
    slope = (grad_band * sigma * (1.0 + mixed * (1.0 - sigma))).astype(jnp.bfloat16)
    ext_grad = lax.dot_general(
        band_dense, slope, (((0,), (0,)), ((), ())), preferred_element_type=jnp.float32
    )
    rim_terms = jnp.concatenate([ext_grad[:BW], ext_grad[BW + row_count :]], axis=0).astype(
        jnp.bfloat16
    )
    padded = padded_2(rim_terms, (("row", 0),), BW)
    grad_hidden = ext_grad[BW : BW + row_count]
    grad_hidden = grad_hidden.at[:BW].add(padded[:BW].astype(jnp.float32))
    grad_hidden = grad_hidden.at[row_count - BW :].add(padded[3 * BW :].astype(jnp.float32))
    owner_terms = jnp.dot(
        jnp.concatenate([dense_high_t, dense_low_t], axis=1),
        jnp.concatenate([slope, slope], axis=0),
        preferred_element_type=jnp.float32,
    )
    to_owner = owner_terms.astype(jnp.bfloat16).reshape(peers, tile_size, width_feat)
    returned = lax.all_to_all(to_owner, "col", split_axis=0, concat_axis=0, tiled=True)
    block_onehot = (giving[None, :] == tile_range[:, None]).astype(jnp.bfloat16)
    from_peers = jnp.einsum(
        "bs,saf->baf", block_onehot, returned, preferred_element_type=jnp.float32
    )
    grad_hidden = grad_hidden + from_peers.reshape(row_count, width_feat)
    grad_round = grad_hidden.astype(jnp.bfloat16)
    partial_weight = lax.dot_general(
        x_band, grad_round, (((0,), (0,)), ((), ())), preferred_element_type=jnp.float32
    )
    nodes_all = row_count * lax.axis_size("row") * peers
    weight_grad = spread_sum(partial_weight, ("row", "col"), nodes_all ** (-0.5))
    feat_band = lax.dot_general(
        grad_round, weight, (((1,), (1,)), ((), ())), preferred_element_type=jnp.float32
    ).astype(jnp.bfloat16)
    feat_grad = lax.dot_general(
        band_perm, feat_band, contract_rows, preferred_element_type=jnp.float32
    ).astype(jnp.bfloat16)
    return (node_out, feat_grad, weight_grad)


def solution(mesh):
    in_specs = (
        P(("row", "col"), None),
        P(),
        P(("row", "col"), None),
        P(("row", "col"), None, None),
        P(("row", "col"), None),
        P(("row", "col"), None, None),
        P(("row", "col"), None),
        P(("row", "col")),
        P(("row", "col"), None),
        P(("row", "col"), None),
        P(("row", "col"), None),
    )
    out_specs = (P(("row", "col"), None), P(("row", "col"), None), P())
    return jax.shard_map(
        on_device, mesh=mesh, in_specs=in_specs, out_specs=out_specs, check_vma=False
    )
```

```python
import jax
import jax.numpy as jnp
from jax import lax
from jax.sharding import PartitionSpec as P

BW = 256


def padded_2(cells, sides, width):
    for axis, dim in sides:
        count = lax.axis_size(axis)
        head = lax.slice_in_dim(cells, 0, width, axis=dim)
        tail = lax.slice_in_dim(cells, cells.shape[dim] - width, cells.shape[dim], axis=dim)
        cells = jnp.concatenate(
            [
                lax.ppermute(tail, axis, [(i, (i + 1) % count) for i in range(count)]),
                cells,
                lax.ppermute(head, axis, [((i + 1) % count, i) for i in range(count)]),
            ],
            axis=dim,
        )
    return cells


def spread_sum(value, axes, scale):
    count = lax.axis_size(axes)
    if value.shape[0] % count == 0:
        piece = (count, value.shape[0] // count, value.shape[1])
    else:
        piece = (count, value.size // count // 128, 128)
    gathered = lax.all_to_all(value.reshape(piece), axes, 0, 0, tiled=True)
    owned = (jnp.sum(gathered, axis=0, keepdims=True) * scale).astype(jnp.bfloat16)
    copies = jnp.broadcast_to(owned, piece)
    spread = lax.all_to_all(copies, axes, 0, 0, tiled=True)
    return spread.astype(jnp.float32).reshape(value.shape)


def on_device(
    node_feats,
    weight,
    cotangent,
    band_tiles,
    band_coords,
    bound_tiles,
    bound_coords,
    bound_count,
    recv_lists,
    send_lists,
    reorder,
):
    tile_size = band_tiles.shape[1]
    row_count = node_feats.shape[0]
    width_feat = node_feats.shape[1]
    tile_rows = row_count // tile_size
    rim_tiles = BW // tile_size
    col_tiles = tile_rows + 2 * rim_tiles
    ext_count = row_count + 2 * BW
    peers = lax.axis_size("col")
    slot_total = bound_tiles.shape[0]
    order = reorder[0]
    node_range = jnp.arange(row_count, dtype=jnp.int32)
    band_perm = (order[:, None] == node_range[None, :]).astype(jnp.bfloat16)
    contract_rows = (((0,), (0,)), ((), ()))
    x_band = jnp.dot(band_perm, node_feats, preferred_element_type=jnp.float32).astype(
        jnp.bfloat16
    )
    hidden = jnp.dot(x_band, weight, preferred_element_type=jnp.float32).astype(jnp.bfloat16)
    band_row_ids = band_coords[:, 0]
    band_col_ids = band_coords[:, 1]
    band_onehot = (
        (band_row_ids[:, None, None] == jnp.arange(tile_rows, dtype=jnp.int32)[None, :, None])
        & (band_col_ids[:, None, None] == jnp.arange(col_tiles, dtype=jnp.int32)[None, None, :])
    ).astype(jnp.bfloat16)
    band_dense = (
        jnp.einsum("krc,kab->racb", band_onehot, band_tiles, preferred_element_type=jnp.float32)
        .astype(jnp.bfloat16)
        .reshape(row_count, ext_count)
    )
    extended = padded_2(hidden, (("row", 0),), BW)
    mixed = jnp.dot(band_dense, extended, preferred_element_type=jnp.float32)
    blocks = hidden.reshape(tile_rows, tile_size, width_feat)
    giving = send_lists[0]
    tile_range = jnp.arange(tile_rows, dtype=jnp.int32)
    give_onehot = (giving[:, None] == tile_range[None, :]).astype(jnp.bfloat16)
    outgoing = jnp.einsum(
        "sb,baf->saf", give_onehot, blocks, preferred_element_type=jnp.float32
    ).astype(jnp.bfloat16)
    arrived = lax.all_to_all(outgoing, "col", split_axis=0, concat_axis=0, tiled=True)
    owner_range = jnp.arange(peers, dtype=jnp.int32)
    live_slots = jnp.arange(slot_total, dtype=jnp.int32) < bound_count[0]
    bound_row_ids = bound_coords[:, 0]
    bound_owner = bound_coords[:, 1]
    slot_onehot = (
        (bound_row_ids[:, None, None] == tile_range[None, :, None])
        & (bound_owner[:, None, None] == owner_range[None, None, :])
        & live_slots[:, None, None]
    ).astype(jnp.bfloat16)
    bound_dense = jnp.einsum(
        "krs,kab->rasb", slot_onehot, bound_tiles, preferred_element_type=jnp.float32
    ).reshape(row_count, peers * tile_size)
    dense_high = bound_dense.astype(jnp.bfloat16)
    dense_low = (bound_dense - dense_high.astype(jnp.float32)).astype(jnp.bfloat16)
    arrived_rows = arrived.reshape(peers * tile_size, width_feat)
    mixed = mixed + jnp.dot(
        jnp.concatenate([dense_high, dense_low], axis=1),
        jnp.concatenate([arrived_rows, arrived_rows], axis=0),
        preferred_element_type=jnp.float32,
    )
    out_band = jax.nn.silu(mixed).astype(jnp.bfloat16)
    node_out = lax.dot_general(
        band_perm, out_band, contract_rows, preferred_element_type=jnp.float32
    ).astype(jnp.bfloat16)
    grad_band = jnp.dot(band_perm, cotangent, preferred_element_type=jnp.float32)
    sigma = jax.nn.sigmoid(mixed)
    slope = (grad_band * sigma * (1.0 + mixed * (1.0 - sigma))).astype(jnp.bfloat16)
    ext_grad = lax.dot_general(
        band_dense, slope, (((0,), (0,)), ((), ())), preferred_element_type=jnp.float32
    )
    rim_terms = jnp.concatenate([ext_grad[:BW], ext_grad[BW + row_count :]], axis=0).astype(
        jnp.bfloat16
    )
    padded = padded_2(rim_terms, (("row", 0),), BW)
    grad_hidden = ext_grad[BW : BW + row_count]
    grad_hidden = grad_hidden.at[:BW].add(padded[:BW].astype(jnp.float32))
    grad_hidden = grad_hidden.at[row_count - BW :].add(padded[3 * BW :].astype(jnp.float32))
    owner_terms = lax.dot_general(
        jnp.concatenate([dense_high, dense_low], axis=0),
        jnp.concatenate([slope, slope], axis=0),
        contract_rows,
        preferred_element_type=jnp.float32,
    )
    to_owner = owner_terms.astype(jnp.bfloat16).reshape(peers, tile_size, width_feat)
    returned = lax.all_to_all(to_owner, "col", split_axis=0, concat_axis=0, tiled=True)
    block_onehot = (giving[None, :] == tile_range[:, None]).astype(jnp.bfloat16)
    from_peers = jnp.einsum(
        "bs,saf->baf", block_onehot, returned, preferred_element_type=jnp.float32
    )
    grad_hidden = grad_hidden + from_peers.reshape(row_count, width_feat)
    grad_round = grad_hidden.astype(jnp.bfloat16)
    partial_weight = lax.dot_general(
        x_band, grad_round, (((0,), (0,)), ((), ())), preferred_element_type=jnp.float32
    )
    nodes_all = row_count * lax.axis_size("row") * peers
    weight_grad = spread_sum(partial_weight, ("col", "row"), nodes_all ** (-0.5))
    feat_band = lax.dot_general(
        grad_round, weight, (((1,), (1,)), ((), ())), preferred_element_type=jnp.float32
    ).astype(jnp.bfloat16)
    feat_grad = lax.dot_general(
        band_perm, feat_band, contract_rows, preferred_element_type=jnp.float32
    ).astype(jnp.bfloat16)
    return (node_out, feat_grad, weight_grad)


def solution(mesh):
    in_specs = (
        P(("row", "col"), None),
        P(),
        P(("row", "col"), None),
        P(("row", "col"), None, None),
        P(("row", "col"), None),
        P(("row", "col"), None, None),
        P(("row", "col"), None),
        P(("row", "col")),
        P(("row", "col"), None),
        P(("row", "col"), None),
        P(("row", "col"), None),
    )
    out_specs = (P(("row", "col"), None), P(("row", "col"), None), P())
    return jax.shard_map(
        on_device, mesh=mesh, in_specs=in_specs, out_specs=out_specs, check_vma=False
    )
```

```python
import jax
import jax.numpy as jnp
from jax import lax
from jax.sharding import PartitionSpec as P

BW = 256


def padded_2(cells, sides, width):
    for axis, dim in sides:
        count = lax.axis_size(axis)
        head = lax.slice_in_dim(cells, 0, width, axis=dim)
        tail = lax.slice_in_dim(cells, cells.shape[dim] - width, cells.shape[dim], axis=dim)
        cells = jnp.concatenate(
            [
                lax.ppermute(tail, axis, [(i, (i + 1) % count) for i in range(count)]),
                cells,
                lax.ppermute(head, axis, [((i + 1) % count, i) for i in range(count)]),
            ],
            axis=dim,
        )
    return cells


def spread_sum(value, axes, scale):
    count = lax.axis_size(axes)
    if value.shape[0] % count == 0:
        piece = (count, value.shape[0] // count, value.shape[1])
    else:
        piece = (count, value.size // count // 128, 128)
    high = value.astype(jnp.bfloat16)
    low = (value - high.astype(jnp.float32)).astype(jnp.bfloat16)
    split = jnp.concatenate([high.reshape(piece), low.reshape(piece)], axis=1)
    gathered = lax.all_to_all(split, axes, 0, 0, tiled=True).astype(jnp.float32)
    rows = piece[1]
    owned = jnp.sum(gathered[:, :rows] + gathered[:, rows:], axis=0, keepdims=True) * scale
    owned = owned.astype(jnp.bfloat16)
    copies = jnp.broadcast_to(owned, piece)
    spread = lax.all_to_all(copies, axes, 0, 0, tiled=True)
    return spread.astype(jnp.float32).reshape(value.shape)


def on_device(
    node_feats,
    weight,
    cotangent,
    band_tiles,
    band_coords,
    bound_tiles,
    bound_coords,
    bound_count,
    recv_lists,
    send_lists,
    reorder,
):
    tile_size = band_tiles.shape[1]
    row_count = node_feats.shape[0]
    width_feat = node_feats.shape[1]
    tile_rows = row_count // tile_size
    rim_tiles = BW // tile_size
    col_tiles = tile_rows + 2 * rim_tiles
    ext_count = row_count + 2 * BW
    peers = lax.axis_size("col")
    slot_total = bound_tiles.shape[0]
    order = reorder[0]
    node_range = jnp.arange(row_count, dtype=jnp.int32)
    band_perm = (order[:, None] == node_range[None, :]).astype(jnp.bfloat16)
    contract_rows = (((0,), (0,)), ((), ()))
    x_band = jnp.dot(band_perm, node_feats, preferred_element_type=jnp.float32).astype(
        jnp.bfloat16
    )
    hidden = jnp.dot(x_band, weight, preferred_element_type=jnp.float32).astype(jnp.bfloat16)
    band_row_ids = band_coords[:, 0]
    band_col_ids = band_coords[:, 1]
    band_onehot = (
        (band_row_ids[:, None, None] == jnp.arange(tile_rows, dtype=jnp.int32)[None, :, None])
        & (band_col_ids[:, None, None] == jnp.arange(col_tiles, dtype=jnp.int32)[None, None, :])
    ).astype(jnp.bfloat16)
    band_dense = (
        jnp.einsum("krc,kab->racb", band_onehot, band_tiles, preferred_element_type=jnp.float32)
        .astype(jnp.bfloat16)
        .reshape(row_count, ext_count)
    )
    extended = padded_2(hidden, (("row", 0),), BW)
    mixed = jnp.dot(band_dense, extended, preferred_element_type=jnp.float32)
    blocks = hidden.reshape(tile_rows, tile_size, width_feat)
    giving = send_lists[0]
    tile_range = jnp.arange(tile_rows, dtype=jnp.int32)
    give_onehot = (giving[:, None] == tile_range[None, :]).astype(jnp.bfloat16)
    outgoing = jnp.einsum(
        "sb,baf->saf", give_onehot, blocks, preferred_element_type=jnp.float32
    ).astype(jnp.bfloat16)
    arrived = lax.all_to_all(outgoing, "col", split_axis=0, concat_axis=0, tiled=True)
    owner_range = jnp.arange(peers, dtype=jnp.int32)
    live_slots = jnp.arange(slot_total, dtype=jnp.int32) < bound_count[0]
    bound_row_ids = bound_coords[:, 0]
    bound_owner = bound_coords[:, 1]
    slot_onehot = (
        (bound_row_ids[:, None, None] == tile_range[None, :, None])
        & (bound_owner[:, None, None] == owner_range[None, None, :])
        & live_slots[:, None, None]
    ).astype(jnp.bfloat16)
    bound_dense = jnp.einsum(
        "krs,kab->rasb", slot_onehot, bound_tiles, preferred_element_type=jnp.float32
    ).reshape(row_count, peers * tile_size)
    dense_high = bound_dense.astype(jnp.bfloat16)
    dense_low = (bound_dense - dense_high.astype(jnp.float32)).astype(jnp.bfloat16)
    arrived_rows = arrived.reshape(peers * tile_size, width_feat)
    mixed = mixed + jnp.dot(
        jnp.concatenate([dense_high, dense_low], axis=1),
        jnp.concatenate([arrived_rows, arrived_rows], axis=0),
        preferred_element_type=jnp.float32,
    )
    out_band = jax.nn.silu(mixed).astype(jnp.bfloat16)
    node_out = lax.dot_general(
        band_perm, out_band, contract_rows, preferred_element_type=jnp.float32
    ).astype(jnp.bfloat16)
    grad_band = jnp.dot(band_perm, cotangent, preferred_element_type=jnp.float32)
    sigma = jax.nn.sigmoid(mixed)
    slope = (grad_band * sigma * (1.0 + mixed * (1.0 - sigma))).astype(jnp.bfloat16)
    ext_grad = lax.dot_general(
        band_dense, slope, (((0,), (0,)), ((), ())), preferred_element_type=jnp.float32
    )
    rim_terms = jnp.concatenate([ext_grad[:BW], ext_grad[BW + row_count :]], axis=0).astype(
        jnp.bfloat16
    )
    padded = padded_2(rim_terms, (("row", 0),), BW)
    grad_hidden = ext_grad[BW : BW + row_count]
    grad_hidden = grad_hidden.at[:BW].add(padded[:BW].astype(jnp.float32))
    grad_hidden = grad_hidden.at[row_count - BW :].add(padded[3 * BW :].astype(jnp.float32))
    owner_terms = lax.dot_general(
        jnp.concatenate([dense_high, dense_low], axis=0),
        jnp.concatenate([slope, slope], axis=0),
        contract_rows,
        preferred_element_type=jnp.float32,
    )
    to_owner = owner_terms.astype(jnp.bfloat16).reshape(peers, tile_size, width_feat)
    returned = lax.all_to_all(to_owner, "col", split_axis=0, concat_axis=0, tiled=True)
    block_onehot = (giving[None, :] == tile_range[:, None]).astype(jnp.bfloat16)
    from_peers = jnp.einsum(
        "bs,saf->baf", block_onehot, returned, preferred_element_type=jnp.float32
    )
    grad_hidden = grad_hidden + from_peers.reshape(row_count, width_feat)
    grad_round = grad_hidden.astype(jnp.bfloat16)
    partial_weight = lax.dot_general(
        x_band, grad_round, (((0,), (0,)), ((), ())), preferred_element_type=jnp.float32
    )
    nodes_all = row_count * lax.axis_size("row") * peers
    weight_grad = spread_sum(partial_weight, ("row", "col"), nodes_all ** (-0.5))
    feat_band = lax.dot_general(
        grad_round, weight, (((1,), (1,)), ((), ())), preferred_element_type=jnp.float32
    ).astype(jnp.bfloat16)
    feat_grad = lax.dot_general(
        band_perm, feat_band, contract_rows, preferred_element_type=jnp.float32
    ).astype(jnp.bfloat16)
    return (node_out, feat_grad, weight_grad)


def solution(mesh):
    in_specs = (
        P(("row", "col"), None),
        P(),
        P(("row", "col"), None),
        P(("row", "col"), None, None),
        P(("row", "col"), None),
        P(("row", "col"), None, None),
        P(("row", "col"), None),
        P(("row", "col")),
        P(("row", "col"), None),
        P(("row", "col"), None),
        P(("row", "col"), None),
    )
    out_specs = (P(("row", "col"), None), P(("row", "col"), None), P())
    return jax.shard_map(
        on_device, mesh=mesh, in_specs=in_specs, out_specs=out_specs, check_vma=False
    )
```

```python
import jax
import jax.numpy as jnp
from jax import lax
from jax.sharding import PartitionSpec as P

BW = 256


def padded_2(cells, sides, width):
    for axis, dim in sides:
        count = lax.axis_size(axis)
        head = lax.slice_in_dim(cells, 0, width, axis=dim)
        tail = lax.slice_in_dim(cells, cells.shape[dim] - width, cells.shape[dim], axis=dim)
        cells = jnp.concatenate(
            [
                lax.ppermute(tail, axis, [(i, (i + 1) % count) for i in range(count)]),
                cells,
                lax.ppermute(head, axis, [((i + 1) % count, i) for i in range(count)]),
            ],
            axis=dim,
        )
    return cells


def spread_sum(value, axes, scale):
    count = lax.axis_size(axes)
    if value.shape[0] % count == 0:
        piece = (count, value.shape[0] // count, value.shape[1])
    else:
        piece = (count, value.size // count // 128, 128)
    high = value.astype(jnp.bfloat16)
    low = (value - high.astype(jnp.float32)).astype(jnp.bfloat16)
    split = jnp.concatenate([high.reshape(piece), low.reshape(piece)], axis=1)
    gathered = lax.all_to_all(split, axes, 0, 0, tiled=True).astype(jnp.float32)
    rows = piece[1]
    owned = jnp.sum(gathered[:, :rows] + gathered[:, rows:], axis=0, keepdims=True) * scale
    owned = owned.astype(jnp.bfloat16)
    copies = jnp.broadcast_to(owned, piece)
    spread = lax.all_to_all(copies, axes, 0, 0, tiled=True)
    return spread.astype(jnp.float32).reshape(value.shape)


def on_device(
    node_feats,
    weight,
    cotangent,
    band_tiles,
    band_coords,
    bound_tiles,
    bound_coords,
    bound_count,
    recv_lists,
    send_lists,
    reorder,
):
    tile_size = band_tiles.shape[1]
    row_count = node_feats.shape[0]
    width_feat = node_feats.shape[1]
    tile_rows = row_count // tile_size
    rim_tiles = BW // tile_size
    col_tiles = tile_rows + 2 * rim_tiles
    ext_count = row_count + 2 * BW
    peers = lax.axis_size("col")
    slot_total = bound_tiles.shape[0]
    order = reorder[0]
    node_range = jnp.arange(row_count, dtype=jnp.int32)
    band_perm = (order[:, None] == node_range[None, :]).astype(jnp.bfloat16)
    contract_rows = (((0,), (0,)), ((), ()))
    x_band = jnp.dot(band_perm, node_feats, preferred_element_type=jnp.float32).astype(
        jnp.bfloat16
    )
    hidden = jnp.dot(x_band, weight, preferred_element_type=jnp.float32).astype(jnp.bfloat16)
    band_row_ids = band_coords[:, 0]
    band_col_ids = band_coords[:, 1]
    band_onehot = (
        (band_row_ids[:, None, None] == jnp.arange(tile_rows, dtype=jnp.int32)[None, :, None])
        & (band_col_ids[:, None, None] == jnp.arange(col_tiles, dtype=jnp.int32)[None, None, :])
    ).astype(jnp.bfloat16)
    band_dense = (
        jnp.einsum("krc,kab->racb", band_onehot, band_tiles, preferred_element_type=jnp.float32)
        .astype(jnp.bfloat16)
        .reshape(row_count, ext_count)
    )
    extended = padded_2(hidden, (("row", 0),), BW)
    mixed = jnp.dot(band_dense, extended, preferred_element_type=jnp.float32)
    blocks = hidden.reshape(tile_rows, tile_size, width_feat)
    giving = send_lists[0]
    tile_range = jnp.arange(tile_rows, dtype=jnp.int32)
    give_onehot = (giving[:, None] == tile_range[None, :]).astype(jnp.bfloat16)
    outgoing = jnp.einsum(
        "sb,baf->saf", give_onehot, blocks, preferred_element_type=jnp.float32
    ).astype(jnp.bfloat16)
    arrived = lax.all_to_all(outgoing, "col", split_axis=0, concat_axis=0, tiled=True)
    owner_range = jnp.arange(peers, dtype=jnp.int32)
    live_slots = jnp.arange(slot_total, dtype=jnp.int32) < bound_count[0]
    bound_row_ids = bound_coords[:, 0]
    bound_owner = bound_coords[:, 1]
    slot_onehot = (
        (bound_row_ids[:, None, None] == tile_range[None, :, None])
        & (bound_owner[:, None, None] == owner_range[None, None, :])
        & live_slots[:, None, None]
    ).astype(jnp.bfloat16)
    bound_dense = jnp.einsum(
        "krs,kab->rasb", slot_onehot, bound_tiles, preferred_element_type=jnp.float32
    ).reshape(row_count, peers * tile_size)
    dense_high = bound_dense.astype(jnp.bfloat16)
    dense_low = (bound_dense - dense_high.astype(jnp.float32)).astype(jnp.bfloat16)
    bound_dense_t = jnp.einsum(
        "krs,kab->sbra", slot_onehot, bound_tiles, preferred_element_type=jnp.float32
    ).reshape(peers * tile_size, row_count)
    dense_high_t = bound_dense_t.astype(jnp.bfloat16)
    dense_low_t = (bound_dense_t - dense_high_t.astype(jnp.float32)).astype(jnp.bfloat16)
    arrived_rows = arrived.reshape(peers * tile_size, width_feat)
    mixed = mixed + jnp.dot(
        jnp.concatenate([dense_high, dense_low], axis=1),
        jnp.concatenate([arrived_rows, arrived_rows], axis=0),
        preferred_element_type=jnp.float32,
    )
    out_band = jax.nn.silu(mixed).astype(jnp.bfloat16)
    node_out = lax.dot_general(
        band_perm, out_band, contract_rows, preferred_element_type=jnp.float32
    ).astype(jnp.bfloat16)
    grad_band = jnp.dot(band_perm, cotangent, preferred_element_type=jnp.float32)
    sigma = jax.nn.sigmoid(mixed)
    slope = (grad_band * sigma * (1.0 + mixed * (1.0 - sigma))).astype(jnp.bfloat16)
    ext_grad = lax.dot_general(
        band_dense, slope, (((0,), (0,)), ((), ())), preferred_element_type=jnp.float32
    )
    rim_terms = jnp.concatenate([ext_grad[:BW], ext_grad[BW + row_count :]], axis=0).astype(
        jnp.bfloat16
    )
    padded = padded_2(rim_terms, (("row", 0),), BW)
    grad_hidden = ext_grad[BW : BW + row_count]
    grad_hidden = grad_hidden.at[:BW].add(padded[:BW].astype(jnp.float32))
    grad_hidden = grad_hidden.at[row_count - BW :].add(padded[3 * BW :].astype(jnp.float32))
    owner_terms = jnp.dot(
        jnp.concatenate([dense_high_t, dense_low_t], axis=1),
        jnp.concatenate([slope, slope], axis=0),
        preferred_element_type=jnp.float32,
    )
    to_owner = owner_terms.astype(jnp.bfloat16).reshape(peers, tile_size, width_feat)
    returned = lax.all_to_all(to_owner, "col", split_axis=0, concat_axis=0, tiled=True)
    block_onehot = (giving[None, :] == tile_range[:, None]).astype(jnp.bfloat16)
    from_peers = jnp.einsum(
        "bs,saf->baf", block_onehot, returned, preferred_element_type=jnp.float32
    )
    grad_hidden = grad_hidden + from_peers.reshape(row_count, width_feat)
    grad_round = grad_hidden.astype(jnp.bfloat16)
    partial_weight = lax.dot_general(
        x_band, grad_round, (((0,), (0,)), ((), ())), preferred_element_type=jnp.float32
    )
    nodes_all = row_count * lax.axis_size("row") * peers
    weight_grad = spread_sum(partial_weight, ("row", "col"), nodes_all ** (-0.5))
    feat_band = lax.dot_general(
        grad_round, weight, (((1,), (1,)), ((), ())), preferred_element_type=jnp.float32
    ).astype(jnp.bfloat16)
    feat_grad = lax.dot_general(
        band_perm, feat_band, contract_rows, preferred_element_type=jnp.float32
    ).astype(jnp.bfloat16)
    return (node_out, feat_grad, weight_grad)


def solution(mesh):
    in_specs = (
        P(("row", "col"), None),
        P(),
        P(("row", "col"), None),
        P(("row", "col"), None, None),
        P(("row", "col"), None),
        P(("row", "col"), None, None),
        P(("row", "col"), None),
        P(("row", "col")),
        P(("row", "col"), None),
        P(("row", "col"), None),
        P(("row", "col"), None),
    )
    out_specs = (P(("row", "col"), None), P(("row", "col"), None), P())
    return jax.shard_map(
        on_device, mesh=mesh, in_specs=in_specs, out_specs=out_specs, check_vma=False
    )
```
